128 devices in a mesh: vx: 16 (over z, x), vy: 8 (over y, core).
Axes of the slice: x: 4, y: 4, z: 4, core: 2. Of those that a mesh axis runs over, the one named last changes fastest.
Arguments:
- fields: bfloat16 [4, 1024, 1280, 128], P(None, 'vx', 'vy'), may hold values from -6 to 6
- modulus: bfloat16 [1024, 1280, 128], P('vx', 'vy'), as said below
- anchors: int32 [16, 8, 14, 3], P('vx', 'vy'), may hold values from 0 to 10, as said below
- home_count: int32 [16, 8], P('vx', 'vy'), may hold values from 1 to 14, as said below
Outputs:
- gradient: float32 [1024, 1280, 128], P('vx', 'vy')
The draws below stay inside these ranges and needn't reach their ends.
Inputs may be any that keep to these rules, and one draw needn't show every extreme that they name: `anchors`: column 0 is at most 4, column 1 at most 10, column 2 at most 2. `home_count`: the counts of the 16 tiles that share a vy index sum to 112. The modulus's real parts are positive and at least three times its imaginary parts, which are positive.
All inputs are finite; a program needn't handle non-finite values.
Results may differ from the reference program's by a relative error of at most 0.0003.
Values may be sent and summed in bfloat16 or wider, within the bound.
No kernel may reach another device: no remote copies, remote signals or barrier semaphores. Data moves between devices by JAX's collectives and lax.ppermute only.
A program may use at most 192 MiB of HBM per device.

```python
import jax
import jax.numpy as jnp
from jax import lax

NF = 4
SUB = 32
HALO = 16
TX = 64
TY = 160
NZ = 64
HOME = 14
WORK = 7
RFWD = 3
NX = 1024
NY = 1280
N_VX = 16
N_VY = 8


def draw_modulus(key, part):
    first, second = jax.random.split(jax.random.fold_in(key, 11))
    real = jax.random.uniform(first, (NX, NY, NZ), jnp.float32, 0.5, 1.5)
    imag = real * jax.random.uniform(second, (NX, NY, NZ), jnp.float32, 0.1, 0.33)
    return jnp.concatenate([real, imag], axis=-1).astype(jnp.bfloat16)


def draw_anchors(key, part):
    keys = jax.random.split(jax.random.fold_in(key, 23), 3)
    across = jax.random.randint(keys[0], (N_VX, N_VY, HOME), 0, TX // HALO + 1)
    along = jax.random.randint(keys[1], (N_VX, N_VY, HOME), 0, TY // HALO + 1)
    depth = jax.random.randint(keys[2], (N_VX, N_VY, HOME), 0, NZ // HALO - 1)
    across = across.at[:, :, 0].set(TX // HALO)
    along = along.at[:, :, 0].set(TY // HALO)
    return jnp.stack([across, along, depth], axis=-1).astype(jnp.int32)


def draw_home_count(key, part):
    first, second = jax.random.split(jax.random.fold_in(key, 37))
    others = N_VX - 1
    rest = N_VX * WORK - HOME
    base = rest // others
    extra = rest % others
    values = jnp.concatenate([jnp.full((1,), HOME, jnp.int32), base + (jnp.arange(others) < extra).astype(jnp.int32)])
    values = jnp.broadcast_to(values[:, None], (N_VX, N_VY))
    pairs = others // 2
    shifts = jax.random.randint(first, (pairs, N_VY), 0, base)
    values = values.at[1:1 + 2 * pairs:2].add(-shifts)
    values = values.at[2:2 + 2 * pairs:2].add(shifts)
    scores = jax.random.randint(second, (N_VX, N_VY), 0, 2 ** 20) * N_VX + jnp.arange(N_VX, dtype=jnp.int32)[:, None]
    order = jnp.argsort(scores, axis=0)
    return jnp.take_along_axis(values, order, axis=0).astype(jnp.int32)


def levels(rng, extent, shards, least, top_value):
    def one(position, blocks):
        draws = jax.random.uniform(jax.random.fold_in(jax.random.fold_in(rng, 6), position), (blocks,), jnp.float32, least / len(shards), top_value / len(shards))
        return jnp.repeat(jnp.exp(draws), extent[position] // blocks).reshape((-1,) + (1,) * (len(extent) - position - 1))

    loudness = one(*shards[0])
    for cut in shards[1:]:
        loudness = loudness * one(*cut)
    return loudness


def normal_values(key, dims, deviation, reach, cuts=(), kind=jnp.bfloat16):
    entries = jax.random.normal(key, dims, jnp.float32) * deviation
    if len(cuts) > 0:
        entries = levels(key, dims, cuts, -0.22, 0.18) * entries
    return jnp.clip(entries, min=-reach, max=reach).astype(kind)


def setup_inputs(seed: int = 0) -> dict:
    seeds = jax.random.split(jax.random.key(seed), 5)
    return {
        "fields": normal_values(seeds[0], (NF, NX, NY, 2 * NZ), 1.0, 6.0, ((1, 16), (2, 8))),
        "modulus": draw_modulus(jax.random.fold_in(seeds[4], 71), 0),
        "anchors": draw_anchors(jax.random.fold_in(seeds[4], 71), 0),
        "home_count": draw_home_count(jax.random.fold_in(seeds[4], 71), 0),
    }


OMEGA = 0.07

def laplace(field):
    padded = jnp.pad(field, ((0, 0), (1, 1), (1, 1), (0, 0), (1, 1)))
    beside = padded[:, 2:, 1:-1, :, 1:-1] + padded[:, :-2, 1:-1, :, 1:-1]
    beside = beside + padded[:, 1:-1, 2:, :, 1:-1] + padded[:, 1:-1, :-2, :, 1:-1]
    beside = beside + padded[:, 1:-1, 1:-1, :, 2:] + padded[:, 1:-1, 1:-1, :, :-2]
    return 6.0 * field - beside

def cmul(left, right):
    real = left[..., 0, :] * right[..., 0, :] - left[..., 1, :] * right[..., 1, :]
    imag = left[..., 0, :] * right[..., 1, :] + left[..., 1, :] * right[..., 0, :]
    return jnp.stack([real, imag], axis=-2)

def conjugate(value):
    return jnp.stack([value[..., 0, :], -value[..., 1, :]], axis=-2)

def subzone_grad(block):
    measured = block[:-1]
    stiff = block[-1:]
    stiff_conj = conjugate(stiff)
    forward = jnp.zeros_like(measured)
    images = []
    for sweep in range(RFWD):
        image = laplace(forward)
        images.append(image)
        forward = forward + OMEGA * (measured - forward - cmul(stiff, image))
    adjoint = forward - measured
    result = jnp.zeros_like(measured[0])
    for sweep in range(RFWD - 1, 0, -1):
        result = result - OMEGA * lax.optimization_barrier(jnp.sum(cmul(adjoint, conjugate(images[sweep])), axis=0))
        if sweep > 1:
            adjoint = adjoint - OMEGA * (adjoint + laplace(cmul(stiff_conj, adjoint)))
    return result

def reference(fields, modulus, anchors, home_count):
    data = jnp.concatenate([fields, modulus[None]], axis=0)
    data = jnp.pad(data, ((0, 0), (HALO, HALO), (HALO, HALO), (0, 0)))
    data = data.reshape(NF + 1, NX + 2 * HALO, NY + 2 * HALO, 2, NZ)
    slots = jnp.arange(HOME, dtype=jnp.int32)
    live = slots[None, None, :] < home_count[:, :, None]
    rows = jnp.arange(N_VX, dtype=jnp.int32)[:, None, None] * TX + HALO * anchors[..., 0]
    cols = jnp.arange(N_VY, dtype=jnp.int32)[None, :, None] * TY + HALO * anchors[..., 1]
    depth = HALO * anchors[..., 2]
    corners = jnp.stack([rows, cols, depth], axis=-1).reshape(-1, 3).astype(jnp.int32)
    order = jnp.argsort(jnp.where(live.reshape(-1), 0, 1).astype(jnp.int32), stable=True)
    corners = corners[order[:N_VX * N_VY * WORK]]
    zero = jnp.zeros((), jnp.int32)

    def one(corner):
        block = lax.dynamic_slice(data, (zero, corner[0], corner[1], zero, corner[2]), (NF + 1, SUB, SUB, 2, SUB))
        return subzone_grad(block.astype(jnp.float32))
    grads = lax.map(one, corners, batch_size=32)
    total = jnp.zeros((NX + 2 * HALO, NY + 2 * HALO, 2, NZ), jnp.float32)

    def deposit(index, total):
        corner = corners[index]
        start = (corner[0], corner[1], zero, corner[2])
        current = lax.dynamic_slice(total, start, (SUB, SUB, 2, SUB))
        return lax.dynamic_update_slice(total, current + grads[index], start)
    total = lax.fori_loop(0, N_VX * N_VY * WORK, deposit, total)
    return total[HALO:HALO + NX, HALO:HALO + NY].reshape(NX, NY, 2 * NZ)
```

```python
import functools

import jax
import jax.numpy as jnp
from jax import lax
from jax.experimental import pallas as pl
from jax.experimental.pallas import tpu as pltpu
from jax.sharding import PartitionSpec as P

NF = 4
SUB = 32
HALO = 16
TX = 64
TY = 160
RFWD = 3


OMEGA = 0.07
PADY = 8


def with_halo(x, sides, width):
    for axis, dim in sides:
        size, length = (lax.axis_size(axis), x.shape[dim])
        up = [(i, (i + 1) % size) for i in range(size - 1)]
        down = [(j, i) for i, j in up]
        last = lax.slice_in_dim(x, length - width, length, axis=dim)
        first = lax.slice_in_dim(x, 0, width, axis=dim)
        before = lax.ppermute(last, axis, up)
        after = lax.ppermute(first, axis, down)
        x = jnp.concatenate([before, x, after], axis=dim)
    return x


def passed_along(x, axis, by):
    length = lax.axis_size(axis)
    pairs = [(i, i + by) for i in range(length) if 0 <= i + by < length]
    return lax.ppermute(x, axis, pairs)


def subzone_kernel(spots_ref, count_ref, block_ref, total_ref,
                   um_ref, mur_ref, muis_ref, w1_ref, w2_ref, t_ref,
                   img1_ref, s1_ref, v3_ref, p_ref, q_ref):
    slot = pl.program_id(0)
    lanes = block_ref.shape[-1]
    half = lanes // 2

    @pl.when(slot == 0)
    def _():
        total_ref[...] = jnp.zeros_like(total_ref)
        w1_ref[...] = jnp.zeros_like(w1_ref)
        w2_ref[...] = jnp.zeros_like(w2_ref)
        t_ref[...] = jnp.zeros_like(t_ref)

    @pl.when(slot < count_ref[0])
    def _():
        x0 = spots_ref[slot, 0]
        y0 = pl.multiple_of(spots_ref[slot, 1], HALO)
        z0 = spots_ref[slot, 2]
        lane = lax.broadcasted_iota(jnp.int32, (SUB, lanes), 1)
        depth = lane % half
        window = (depth >= z0) & (depth < z0 + SUB)
        upper = lane >= half

        def swap(v):
            return pltpu.roll(v, half, 1)

        def laplace(ref, f, x):
            c = ref[f, x + 1, PADY:PADY + SUB, :]
            side = ref[f, x, PADY:PADY + SUB, :] + ref[f, x + 2, PADY:PADY + SUB, :]
            side = side + ref[f, x + 1, PADY - 1:PADY - 1 + SUB, :]
            side = side + ref[f, x + 1, PADY + 1:PADY + 1 + SUB, :]
            side = side + pltpu.roll(c, 1, 1) + pltpu.roll(c, lanes - 1, 1)
            return 6.0 * c - side, c

        def stage_a(x, carry):
            mu = jnp.where(window, block_ref[NF, x].astype(jnp.float32), 0.0)
            smu = swap(mu)
            mur_ref[x] = jnp.where(upper, smu, mu)
            muis_ref[x] = jnp.where(upper, mu, -smu)
            for f in range(NF):
                u = jnp.where(window, block_ref[f, x].astype(jnp.float32), 0.0)
                um_ref[f, x] = u
                w1_ref[f, x + 1, PADY:PADY + SUB, :] = OMEGA * u
            return carry

        lax.fori_loop(0, SUB, stage_a, 0)

        def stage_b(x, carry):
            mur = mur_ref[x]
            muis = muis_ref[x]
            for f in range(NF):
                img, c = laplace(w1_ref, f, x)
                s = swap(img)
                u = um_ref[f, x]
                w2_ref[f, x + 1, PADY:PADY + SUB, :] = c + OMEGA * (u - c - (mur * img + muis * s))
                img1_ref[f, x] = img
                s1_ref[f, x] = s
            return carry

        lax.fori_loop(0, SUB, stage_b, 0)

        def stage_c(x, carry):
            mur = mur_ref[x]
            muis = muis_ref[x]
            pacc = jnp.zeros((SUB, lanes), jnp.float32)
            qacc = jnp.zeros((SUB, lanes), jnp.float32)
            for f in range(NF):
                img, c = laplace(w2_ref, f, x)
                s = swap(img)
                u = um_ref[f, x]
                w3 = c + OMEGA * (u - c - (mur * img + muis * s))
                v3 = w3 - u
                t_ref[f, x + 1, PADY:PADY + SUB, :] = mur * v3 - muis * swap(v3)
                v3_ref[f, x] = v3
                pacc = pacc + v3 * img
                qacc = qacc + v3 * s
            p_ref[x] = pacc
            q_ref[x] = qacc
            return carry

        lax.fori_loop(0, SUB, stage_c, 0)

        def stage_d(x, carry):
            pacc = p_ref[x]
            qacc = q_ref[x]
            for f in range(NF):
                lt, _ = laplace(t_ref, f, x)
                v3 = v3_ref[f, x]
                v2 = v3 - OMEGA * (v3 + lt)
                pacc = pacc + v2 * img1_ref[f, x]
                qacc = qacc + v2 * s1_ref[f, x]
            res = jnp.where(upper, qacc - swap(qacc), pacc + swap(pacc))
            res = jnp.where(window, -OMEGA * res, 0.0)
            total_ref[x0 + x, pl.ds(y0, SUB), :] += res
            return carry

        lax.fori_loop(0, SUB, stage_d, 0)


def subzone_pass(extended, spots, count):
    lanes = extended.shape[-1]
    home = spots.shape[0]
    ex, ey = extended.shape[1], extended.shape[2]

    def block_map(s, spots_ref, count_ref):
        live = jnp.minimum(s, jnp.maximum(count_ref[0] - 1, 0))
        return (0, spots_ref[live, 0], pl.multiple_of(spots_ref[live, 1], HALO), 0)

    f32 = jnp.float32
    padded = (NF, SUB + 2, SUB + 2 * PADY, lanes)
    grid_spec = pltpu.PrefetchScalarGridSpec(
        num_scalar_prefetch=2,
        grid=(home,),
        in_specs=[pl.BlockSpec((pl.Element(NF + 1), pl.Element(SUB), pl.Element(SUB), pl.Element(lanes)), block_map)],
        out_specs=pl.BlockSpec((ex, ey, lanes), lambda s, spots_ref, count_ref: (0, 0, 0)),
        scratch_shapes=[
            pltpu.VMEM((NF, SUB, SUB, lanes), f32),
            pltpu.VMEM((SUB, SUB, lanes), f32),
            pltpu.VMEM((SUB, SUB, lanes), f32),
            pltpu.VMEM(padded, f32),
            pltpu.VMEM(padded, f32),
            pltpu.VMEM(padded, f32),
            pltpu.VMEM((NF, SUB, SUB, lanes), f32),
            pltpu.VMEM((NF, SUB, SUB, lanes), f32),
            pltpu.VMEM((NF, SUB, SUB, lanes), f32),
            pltpu.VMEM((SUB, SUB, lanes), f32),
            pltpu.VMEM((SUB, SUB, lanes), f32),
        ],
    )
    return pl.pallas_call(
        subzone_kernel,
        grid_spec=grid_spec,
        out_shape=jax.ShapeDtypeStruct((ex, ey, lanes), f32),
        compiler_params=pltpu.CompilerParams(
            dimension_semantics=("arbitrary",), vmem_limit_bytes=100 * 1024 * 1024
        ),
    )(spots, count, extended)


def shards(fields, modulus, anchors, home_count):
    data = jnp.concatenate([fields, modulus[None]], axis=0)
    extended = with_halo(data, (("vx", 1), ("vy", 2)), HALO)
    spots = (anchors[0, 0] * HALO).astype(jnp.int32)
    count = home_count[0].astype(jnp.int32)
    total = subzone_pass(extended, spots, count)
    from_above = passed_along(total[:HALO], "vx", -1)
    from_below = passed_along(total[TX + HALO :], "vx", 1)
    middle = total[HALO : HALO + TX]
    middle = middle.at[:HALO].add(from_below).at[TX - HALO :].add(from_above)
    from_right = passed_along(middle[:, :HALO], "vy", -1)
    from_left = passed_along(middle[:, TY + HALO :], "vy", 1)
    owned = middle[:, HALO : HALO + TY]
    owned = owned.at[:, :HALO].add(from_left).at[:, TY - HALO :].add(from_right)
    return owned


def solution(mesh):
    return jax.shard_map(
        shards,
        mesh=mesh,
        in_specs=(
            P(None, "vx", "vy", None),
            P("vx", "vy", None),
            P("vx", "vy", None, None),
            P("vx", "vy"),
        ),
        out_specs=P("vx", "vy", None),
        check_vma=False,
    )
```

```python
import functools

import jax
import jax.numpy as jnp
from jax import lax
from jax.experimental import pallas as pl
from jax.experimental.pallas import tpu as pltpu
from jax.sharding import PartitionSpec as P

NF = 4
SUB = 32
HALO = 16
TX = 64
TY = 160
RFWD = 3


OMEGA = 0.07
PADY = 8


def with_halo(x, sides, width):
    for axis, dim in sides:
        size, length = (lax.axis_size(axis), x.shape[dim])
        up = [(i, (i + 1) % size) for i in range(size - 1)]
        down = [(j, i) for i, j in up]
        last = lax.slice_in_dim(x, length - width, length, axis=dim)
        first = lax.slice_in_dim(x, 0, width, axis=dim)
        before = lax.ppermute(last, axis, up)
        after = lax.ppermute(first, axis, down)
        x = jnp.concatenate([before, x, after], axis=dim)
    return x


def passed_along(x, axis, by):
    length = lax.axis_size(axis)
    pairs = [(i, i + by) for i in range(length) if 0 <= i + by < length]
    return lax.ppermute(x, axis, pairs)


def subzone_kernel(spots_ref, count_ref, block_a, block_b, total_ref,
                   um_ref, mur_ref, muis_ref, w1_ref, w2_ref, t_ref,
                   img1_ref, s1_ref, v3_ref, p_ref, q_ref):
    step = pl.program_id(0)
    lanes = block_a.shape[-1]
    half = lanes // 2
    group = half // 2
    first = 2 * step
    second = jnp.minimum(first + 1, count_ref[0] - 1)

    @pl.when(step == 0)
    def _():
        total_ref[...] = jnp.zeros_like(total_ref)
        w1_ref[...] = jnp.zeros_like(w1_ref)
        w2_ref[...] = jnp.zeros_like(w2_ref)
        t_ref[...] = jnp.zeros_like(t_ref)

    @pl.when(first < count_ref[0])
    def _():
        xa = spots_ref[first, 0]
        ya = pl.multiple_of(spots_ref[first, 1], HALO)
        za = spots_ref[first, 2]
        xb = spots_ref[second, 0]
        yb = pl.multiple_of(spots_ref[second, 1], HALO)
        zb = spots_ref[second, 2]
        lane = lax.broadcasted_iota(jnp.int32, (SUB, lanes), 1)
        depth = lane % half
        in_a = (lane % half) < group
        upper = lane >= half
        not_low = (lane % group) != 0
        not_high = (lane % group) != group - 1
        shift_a = (lanes - za) % lanes
        shift_b = (group - zb + lanes) % lanes

        def swap(v):
            return pltpu.roll(v, half, 1)

        def packed(k, x):
            a = block_a[k, x].astype(jnp.float32)
            b = block_b[k, x].astype(jnp.float32)
            return jnp.where(in_a, pltpu.roll(a, shift_a, 1), pltpu.roll(b, shift_b, 1))

        def laplace(ref, f, x):
            c = ref[f, x + 1, PADY:PADY + SUB, :]
            side = ref[f, x, PADY:PADY + SUB, :] + ref[f, x + 2, PADY:PADY + SUB, :]
            side = side + ref[f, x + 1, PADY - 1:PADY - 1 + SUB, :]
            side = side + ref[f, x + 1, PADY + 1:PADY + 1 + SUB, :]
            side = side + jnp.where(not_low, pltpu.roll(c, 1, 1), 0.0)
            side = side + jnp.where(not_high, pltpu.roll(c, lanes - 1, 1), 0.0)
            return 6.0 * c - side, c

        def stage_a(x, carry):
            mu = packed(NF, x)
            smu = swap(mu)
            mur_ref[x] = jnp.where(upper, smu, mu)
            muis_ref[x] = jnp.where(upper, mu, -smu)
            for f in range(NF):
                u = packed(f, x)
                um_ref[f, x] = u
                w1_ref[f, x + 1, PADY:PADY + SUB, :] = OMEGA * u
            return carry

        lax.fori_loop(0, SUB, stage_a, 0)

        def stage_b(x, carry):
            mur = mur_ref[x]
            muis = muis_ref[x]
            for f in range(NF):
                img, c = laplace(w1_ref, f, x)
                s = swap(img)
                u = um_ref[f, x]
                w2_ref[f, x + 1, PADY:PADY + SUB, :] = c + OMEGA * (u - c - (mur * img + muis * s))
                img1_ref[f, x] = img
                s1_ref[f, x] = s
            return carry

        lax.fori_loop(0, SUB, stage_b, 0)

        def stage_c(x, carry):
            mur = mur_ref[x]
            muis = muis_ref[x]
            pacc = jnp.zeros((SUB, lanes), jnp.float32)
            qacc = jnp.zeros((SUB, lanes), jnp.float32)
            for f in range(NF):
                img, c = laplace(w2_ref, f, x)
                s = swap(img)
                u = um_ref[f, x]
                w3 = c + OMEGA * (u - c - (mur * img + muis * s))
                v3 = w3 - u
                t_ref[f, x + 1, PADY:PADY + SUB, :] = mur * v3 - muis * swap(v3)
                v3_ref[f, x] = v3
                pacc = pacc + v3 * img
                qacc = qacc + v3 * s
            p_ref[x] = pacc
            q_ref[x] = qacc
            return carry

        lax.fori_loop(0, SUB, stage_c, 0)

        window_a = (depth >= za) & (depth < za + SUB)
        window_b = (depth >= zb) & (depth < zb + SUB)
        back_a = za % lanes
        back_b = (zb + lanes - group) % lanes
        live_b = first + 1 < count_ref[0]

        def stage_d(x, carry):
            pacc = p_ref[x]
            qacc = q_ref[x]
            for f in range(NF):
                lt, _ = laplace(t_ref, f, x)
                v3 = v3_ref[f, x]
                v2 = v3 - OMEGA * (v3 + lt)
                pacc = pacc + v2 * img1_ref[f, x]
                qacc = qacc + v2 * s1_ref[f, x]
            res = -OMEGA * jnp.where(upper, qacc - swap(qacc), pacc + swap(pacc))
            total_ref[xa + x, pl.ds(ya, SUB), :] += jnp.where(window_a, pltpu.roll(res, back_a, 1), 0.0)

            @pl.when(live_b)
            def _():
                total_ref[xb + x, pl.ds(yb, SUB), :] += jnp.where(window_b, pltpu.roll(res, back_b, 1), 0.0)

            return carry

        lax.fori_loop(0, SUB, stage_d, 0)


def subzone_pass(extended, spots, count):
    lanes = extended.shape[-1]
    home = spots.shape[0]
    ex, ey = extended.shape[1], extended.shape[2]

    def block_map(offset):
        def index(s, spots_ref, count_ref):
            live = jnp.minimum(2 * s + offset, jnp.maximum(count_ref[0] - 1, 0))
            return (0, spots_ref[live, 0], pl.multiple_of(spots_ref[live, 1], HALO), 0)
        return index

    f32 = jnp.float32
    padded = (NF, SUB + 2, SUB + 2 * PADY, lanes)
    block = (pl.Element(NF + 1), pl.Element(SUB), pl.Element(SUB), pl.Element(lanes))
    grid_spec = pltpu.PrefetchScalarGridSpec(
        num_scalar_prefetch=2,
        grid=((home + 1) // 2,),
        in_specs=[pl.BlockSpec(block, block_map(0)), pl.BlockSpec(block, block_map(1))],
        out_specs=pl.BlockSpec((ex, ey, lanes), lambda s, spots_ref, count_ref: (0, 0, 0)),
        scratch_shapes=[
            pltpu.VMEM((NF, SUB, SUB, lanes), f32),
            pltpu.VMEM((SUB, SUB, lanes), f32),
            pltpu.VMEM((SUB, SUB, lanes), f32),
            pltpu.VMEM(padded, f32),
            pltpu.VMEM(padded, f32),
            pltpu.VMEM(padded, f32),
            pltpu.VMEM((NF, SUB, SUB, lanes), f32),
            pltpu.VMEM((NF, SUB, SUB, lanes), f32),
            pltpu.VMEM((NF, SUB, SUB, lanes), f32),
            pltpu.VMEM((SUB, SUB, lanes), f32),
            pltpu.VMEM((SUB, SUB, lanes), f32),
        ],
    )
    return pl.pallas_call(
        subzone_kernel,
        grid_spec=grid_spec,
        out_shape=jax.ShapeDtypeStruct((ex, ey, lanes), f32),
        compiler_params=pltpu.CompilerParams(
            dimension_semantics=("arbitrary",), vmem_limit_bytes=100 * 1024 * 1024
        ),
    )(spots, count, extended, extended)


def shards(fields, modulus, anchors, home_count):
    data = jnp.concatenate([fields, modulus[None]], axis=0)
    extended = with_halo(data, (("vx", 1), ("vy", 2)), HALO)
    spots = (anchors[0, 0] * HALO).astype(jnp.int32)
    count = home_count[0].astype(jnp.int32)
    total = subzone_pass(extended, spots, count)
    from_above = passed_along(total[:HALO], "vx", -1)
    from_below = passed_along(total[TX + HALO :], "vx", 1)
    middle = total[HALO : HALO + TX]
    middle = middle.at[:HALO].add(from_below).at[TX - HALO :].add(from_above)
    from_right = passed_along(middle[:, :HALO], "vy", -1)
    from_left = passed_along(middle[:, TY + HALO :], "vy", 1)
    owned = middle[:, HALO : HALO + TY]
    owned = owned.at[:, :HALO].add(from_left).at[:, TY - HALO :].add(from_right)
    return owned


def solution(mesh):
    return jax.shard_map(
        shards,
        mesh=mesh,
        in_specs=(
            P(None, "vx", "vy", None),
            P("vx", "vy", None),
            P("vx", "vy", None, None),
            P("vx", "vy"),
        ),
        out_specs=P("vx", "vy", None),
        check_vma=False,
    )
```

```python
import functools

import jax
import jax.numpy as jnp
from jax import lax
from jax.experimental import pallas as pl
from jax.experimental.pallas import tpu as pltpu
from jax.sharding import PartitionSpec as P

NF = 4
SUB = 32
HALO = 16
TX = 64
TY = 160
RFWD = 3


OMEGA = 0.07
PADY = 8


def shifted(x, by_x, by_y):
    nx, ny = lax.axis_size("vx"), lax.axis_size("vy")
    pairs = []
    for a in range(nx):
        for b in range(ny):
            if 0 <= a + by_x < nx and 0 <= b + by_y < ny:
                pairs.append((a * ny + b, (a + by_x) * ny + b + by_y))
    return lax.ppermute(x, ("vx", "vy"), pairs)


def with_halo(x, width):
    rows, cols = x.shape[1], x.shape[2]
    top = x[:, rows - width :]
    bottom = x[:, :width]
    xlo = shifted(top, 1, 0)
    xhi = shifted(bottom, -1, 0)
    ylo = shifted(x[:, :, cols - width :], 0, 1)
    yhi = shifted(x[:, :, :width], 0, -1)
    c_ll = shifted(top[:, :, cols - width :], 1, 1)
    c_lh = shifted(top[:, :, :width], 1, -1)
    c_hl = shifted(bottom[:, :, cols - width :], -1, 1)
    c_hh = shifted(bottom[:, :, :width], -1, -1)
    left = jnp.concatenate([c_ll, ylo, c_hl], axis=1)
    right = jnp.concatenate([c_lh, yhi, c_hh], axis=1)
    middle = jnp.concatenate([xlo, x, xhi], axis=1)
    return jnp.concatenate([left, middle, right], axis=2)


def passed_along(x, axis, by):
    length = lax.axis_size(axis)
    pairs = [(i, i + by) for i in range(length) if 0 <= i + by < length]
    return lax.ppermute(x, axis, pairs)


def subzone_kernel(spots_ref, count_ref, block_a, mod_a, block_b, mod_b, total_ref,
                   um_ref, mur_ref, muis_ref, w1_ref, w2_ref, t_ref,
                   img1_ref, s1_ref, v3_ref, p_ref, q_ref):
    step = pl.program_id(0)
    lanes = block_a.shape[-1]
    half = lanes // 2
    group = half // 2
    first = 2 * step
    second = jnp.minimum(first + 1, count_ref[0] - 1)

    @pl.when(step == 0)
    def _():
        total_ref[...] = jnp.zeros_like(total_ref)
        w1_ref[...] = jnp.zeros_like(w1_ref)
        w2_ref[...] = jnp.zeros_like(w2_ref)
        t_ref[...] = jnp.zeros_like(t_ref)

    @pl.when(first < count_ref[0])
    def _():
        xa = spots_ref[first, 0]
        ya = pl.multiple_of(spots_ref[first, 1], HALO)
        za = spots_ref[first, 2]
        xb = spots_ref[second, 0]
        yb = pl.multiple_of(spots_ref[second, 1], HALO)
        zb = spots_ref[second, 2]
        lane = lax.broadcasted_iota(jnp.int32, (SUB, lanes), 1)
        depth = lane % half
        in_a = (lane % half) < group
        upper = lane >= half
        not_low = (lane % group) != 0
        not_high = (lane % group) != group - 1
        shift_a = (lanes - za) % lanes
        shift_b = (group - zb + lanes) % lanes

        def swap(v):
            return pltpu.roll(v, half, 1)

        def packed(ref_a, ref_b, k, x):
            a = ref_a[k, x].astype(jnp.float32)
            b = ref_b[k, x].astype(jnp.float32)
            return jnp.where(in_a, pltpu.roll(a, shift_a, 1), pltpu.roll(b, shift_b, 1))

        def laplace(ref, f, x):
            c = ref[f, x + 1, PADY:PADY + SUB, :]
            side = ref[f, x, PADY:PADY + SUB, :] + ref[f, x + 2, PADY:PADY + SUB, :]
            side = side + ref[f, x + 1, PADY - 1:PADY - 1 + SUB, :]
            side = side + ref[f, x + 1, PADY + 1:PADY + 1 + SUB, :]
            side = side + jnp.where(not_low, pltpu.roll(c, 1, 1), 0.0)
            side = side + jnp.where(not_high, pltpu.roll(c, lanes - 1, 1), 0.0)
            return 6.0 * c - side, c

        def stage_a(x, carry):
            mu = packed(mod_a, mod_b, 0, x)
            smu = swap(mu)
            mur_ref[x] = jnp.where(upper, smu, mu)
            muis_ref[x] = jnp.where(upper, mu, -smu)
            for f in range(NF):
                u = packed(block_a, block_b, f, x)
                um_ref[f, x] = u
                w1_ref[f, x + 1, PADY:PADY + SUB, :] = OMEGA * u
            return carry

        lax.fori_loop(0, SUB, stage_a, 0)

        def stage_b(x, carry):
            mur = mur_ref[x]
            muis = muis_ref[x]
            for f in range(NF):
                img, c = laplace(w1_ref, f, x)
                s = swap(img)
                u = um_ref[f, x]
                w2_ref[f, x + 1, PADY:PADY + SUB, :] = c + OMEGA * (u - c - (mur * img + muis * s))
                img1_ref[f, x] = img
                s1_ref[f, x] = s
            return carry

        lax.fori_loop(0, SUB, stage_b, 0)

        def stage_c(x, carry):
            mur = mur_ref[x]
            muis = muis_ref[x]
            pacc = jnp.zeros((SUB, lanes), jnp.float32)
            qacc = jnp.zeros((SUB, lanes), jnp.float32)
            for f in range(NF):
                img, c = laplace(w2_ref, f, x)
                s = swap(img)
                u = um_ref[f, x]
                w3 = c + OMEGA * (u - c - (mur * img + muis * s))
                v3 = w3 - u
                t_ref[f, x + 1, PADY:PADY + SUB, :] = mur * v3 - muis * swap(v3)
                v3_ref[f, x] = v3
                pacc = pacc + v3 * img
                qacc = qacc + v3 * s
            p_ref[x] = pacc
            q_ref[x] = qacc
            return carry

        lax.fori_loop(0, SUB, stage_c, 0)

        window_a = (depth >= za) & (depth < za + SUB)
        window_b = (depth >= zb) & (depth < zb + SUB)
        back_a = za % lanes
        back_b = (zb + lanes - group) % lanes
        live_b = first + 1 < count_ref[0]

        def stage_d(x, carry):
            pacc = p_ref[x]
            qacc = q_ref[x]
            for f in range(NF):
                lt, _ = laplace(t_ref, f, x)
                v3 = v3_ref[f, x]
                v2 = v3 - OMEGA * (v3 + lt)
                pacc = pacc + v2 * img1_ref[f, x]
                qacc = qacc + v2 * s1_ref[f, x]
            res = -OMEGA * jnp.where(upper, qacc - swap(qacc), pacc + swap(pacc))
            total_ref[xa + x, pl.ds(ya, SUB), :] += jnp.where(window_a, pltpu.roll(res, back_a, 1), 0.0)

            @pl.when(live_b)
            def _():
                total_ref[xb + x, pl.ds(yb, SUB), :] += jnp.where(window_b, pltpu.roll(res, back_b, 1), 0.0)

            return carry

        lax.fori_loop(0, SUB, stage_d, 0)


def subzone_pass(fields, modulus, spots, count, shift, extent):
    lanes = fields.shape[-1]
    home = spots.shape[0]
    ex, ey = extent

    def block_map(offset, base):
        def index(s, spots_ref, count_ref):
            live = jnp.minimum(2 * s + offset, jnp.maximum(count_ref[0] - 1, 0))
            row = jnp.clip(spots_ref[live, 0] - shift, 0, fields.shape[1] - SUB)
            col = jnp.clip(spots_ref[live, 1] - shift, 0, fields.shape[2] - SUB)
            col = pl.multiple_of(col, HALO)
            return (base, row, col, 0)
        return index

    f32 = jnp.float32
    padded = (NF, SUB + 2, SUB + 2 * PADY, lanes)
    block = (pl.Element(NF), pl.Element(SUB), pl.Element(SUB), pl.Element(lanes))
    mod_block = (pl.Element(1), pl.Element(SUB), pl.Element(SUB), pl.Element(lanes))
    base = modulus.shape[0] - 1
    grid_spec = pltpu.PrefetchScalarGridSpec(
        num_scalar_prefetch=2,
        grid=((home + 1) // 2,),
        in_specs=[
            pl.BlockSpec(block, block_map(0, 0)),
            pl.BlockSpec(mod_block, block_map(0, base)),
            pl.BlockSpec(block, block_map(1, 0)),
            pl.BlockSpec(mod_block, block_map(1, base)),
        ],
        out_specs=pl.BlockSpec((ex, ey, lanes), lambda s, spots_ref, count_ref: (0, 0, 0)),
        scratch_shapes=[
            pltpu.VMEM((NF, SUB, SUB, lanes), f32),
            pltpu.VMEM((SUB, SUB, lanes), f32),
            pltpu.VMEM((SUB, SUB, lanes), f32),
            pltpu.VMEM(padded, f32),
            pltpu.VMEM(padded, f32),
            pltpu.VMEM(padded, f32),
            pltpu.VMEM((NF, SUB, SUB, lanes), f32),
            pltpu.VMEM((NF, SUB, SUB, lanes), f32),
            pltpu.VMEM((NF, SUB, SUB, lanes), f32),
            pltpu.VMEM((SUB, SUB, lanes), f32),
            pltpu.VMEM((SUB, SUB, lanes), f32),
        ],
    )
    return pl.pallas_call(
        subzone_kernel,
        grid_spec=grid_spec,
        out_shape=jax.ShapeDtypeStruct((ex, ey, lanes), f32),
        compiler_params=pltpu.CompilerParams(
            dimension_semantics=("arbitrary",), vmem_limit_bytes=100 * 1024 * 1024
        ),
    )(spots, count, fields, modulus, fields, modulus)


def shards(fields, modulus, anchors, home_count):
    home = anchors.shape[2]
    spots = (anchors[0, 0] * HALO).astype(jnp.int32)
    count = home_count[0, 0].astype(jnp.int32)
    slots = jnp.arange(home, dtype=jnp.int32)
    live = slots < count
    inner = (spots[:, 0] >= HALO) & (spots[:, 0] + SUB <= TX + HALO)
    inner = inner & (spots[:, 1] >= HALO) & (spots[:, 1] + SUB <= TY + HALO) & live
    order = jnp.argsort(jnp.where(inner, 0, 1).astype(jnp.int32), stable=True)
    spots = spots[order]
    first = (jnp.sum(inner.astype(jnp.int32)) // 2) * 2
    rest = jnp.take(spots, (slots + first) % home, axis=0)
    extent = (TX + 2 * HALO, TY + 2 * HALO)
    inside = subzone_pass(fields, modulus[None], spots, first[None], HALO, extent)
    data = jnp.concatenate([fields, modulus[None]], axis=0)
    extended = with_halo(data, HALO)
    outside = subzone_pass(extended, extended, rest, (count - first)[None], 0, extent)
    total = inside + outside
    from_above = passed_along(total[:HALO], "vx", -1)
    from_below = passed_along(total[TX + HALO :], "vx", 1)
    middle = total[HALO : HALO + TX]
    middle = middle.at[:HALO].add(from_below).at[TX - HALO :].add(from_above)
    from_right = passed_along(middle[:, :HALO], "vy", -1)
    from_left = passed_along(middle[:, TY + HALO :], "vy", 1)
    owned = middle[:, HALO : HALO + TY]
    owned = owned.at[:, :HALO].add(from_left).at[:, TY - HALO :].add(from_right)
    return owned


def solution(mesh):
    return jax.shard_map(
        shards,
        mesh=mesh,
        in_specs=(
            P(None, "vx", "vy", None),
            P("vx", "vy", None),
            P("vx", "vy", None, None),
            P("vx", "vy"),
        ),
        out_specs=P("vx", "vy", None),
        check_vma=False,
    )
```

```python
import functools

import jax
import jax.numpy as jnp
from jax import lax
from jax.experimental import pallas as pl
from jax.experimental.pallas import tpu as pltpu
from jax.sharding import PartitionSpec as P

NF = 4
SUB = 32
HALO = 16
TX = 64
TY = 160
RFWD = 3


OMEGA = 0.07
PADY = 8


def with_halo(x, sides, width):
    for axis, dim in sides:
        size, length = (lax.axis_size(axis), x.shape[dim])
        up = [(i, (i + 1) % size) for i in range(size - 1)]
        down = [(j, i) for i, j in up]
        last = lax.slice_in_dim(x, length - width, length, axis=dim)
        first = lax.slice_in_dim(x, 0, width, axis=dim)
        before = lax.ppermute(last, axis, up)
        after = lax.ppermute(first, axis, down)
        x = jnp.concatenate([before, x, after], axis=dim)
    return x


def passed_along(x, axis, by):
    length = lax.axis_size(axis)
    pairs = [(i, i + by) for i in range(length) if 0 <= i + by < length]
    return lax.ppermute(x, axis, pairs)


def subzone_kernel(spots_ref, count_ref, block_a, block_b, total_ref,
                   um_ref, mur_ref, muis_ref, w1_ref, w2_ref, t_ref,
                   img1_ref, s1_ref, v3_ref, p_ref, q_ref):
    step = pl.program_id(0)
    lanes = block_a.shape[-1]
    half = lanes // 2
    group = half // 2
    first = 2 * step
    second = jnp.minimum(first + 1, count_ref[0] - 1)

    @pl.when(step == 0)
    def _():
        total_ref[...] = jnp.zeros_like(total_ref)
        w1_ref[...] = jnp.zeros_like(w1_ref)
        w2_ref[...] = jnp.zeros_like(w2_ref)
        t_ref[...] = jnp.zeros_like(t_ref)

    @pl.when(first < count_ref[0])
    def _():
        xa = spots_ref[first, 0]
        ya = pl.multiple_of(spots_ref[first, 1], HALO)
        za = spots_ref[first, 2]
        xb = spots_ref[second, 0]
        yb = pl.multiple_of(spots_ref[second, 1], HALO)
        zb = spots_ref[second, 2]
        lane = lax.broadcasted_iota(jnp.int32, (SUB, lanes), 1)
        depth = lane % half
        in_a = (lane % half) < group
        upper = lane >= half
        not_low = (lane % group) != 0
        not_high = (lane % group) != group - 1
        shift_a = (lanes - za) % lanes
        shift_b = (group - zb + lanes) % lanes

        def swap(v):
            return pltpu.roll(v, half, 1)

        def packed(k, x):
            a = block_a[k, x].astype(jnp.float32)
            b = block_b[k, x].astype(jnp.float32)
            return jnp.where(in_a, pltpu.roll(a, shift_a, 1), pltpu.roll(b, shift_b, 1))

        def laplace(ref, f, x):
            c = ref[f, x + 1, PADY:PADY + SUB, :]
            side = ref[f, x, PADY:PADY + SUB, :] + ref[f, x + 2, PADY:PADY + SUB, :]
            side = side + ref[f, x + 1, PADY - 1:PADY - 1 + SUB, :]
            side = side + ref[f, x + 1, PADY + 1:PADY + 1 + SUB, :]
            side = side + jnp.where(not_low, pltpu.roll(c, 1, 1), 0.0)
            side = side + jnp.where(not_high, pltpu.roll(c, lanes - 1, 1), 0.0)
            return 6.0 * c - side, c

        def stage_a(x, carry):
            mu = packed(NF, x)
            smu = swap(mu)
            mur_ref[x] = jnp.where(upper, smu, mu)
            muis_ref[x] = jnp.where(upper, mu, -smu)
            for f in range(NF):
                u = packed(f, x)
                um_ref[f, x] = u
                w1_ref[f, x + 1, PADY:PADY + SUB, :] = OMEGA * u
            return carry

        lax.fori_loop(0, SUB, stage_a, 0)

        def stage_b(x, carry):
            mur = mur_ref[x]
            muis = muis_ref[x]
            for f in range(NF):
                img, c = laplace(w1_ref, f, x)
                s = swap(img)
                u = um_ref[f, x]
                w2_ref[f, x + 1, PADY:PADY + SUB, :] = c + OMEGA * (u - c - (mur * img + muis * s))
                img1_ref[f, x] = img
                s1_ref[f, x] = s
            return carry

        lax.fori_loop(0, SUB, stage_b, 0)

        def stage_c(x, carry):
            mur = mur_ref[x]
            muis = muis_ref[x]
            pacc = jnp.zeros((SUB, lanes), jnp.float32)
            qacc = jnp.zeros((SUB, lanes), jnp.float32)
            for f in range(NF):
                img, c = laplace(w2_ref, f, x)
                s = swap(img)
                u = um_ref[f, x]
                w3 = c + OMEGA * (u - c - (mur * img + muis * s))
                v3 = w3 - u
                t_ref[f, x + 1, PADY:PADY + SUB, :] = mur * v3 - muis * swap(v3)
                v3_ref[f, x] = v3
                pacc = pacc + v3 * img
                qacc = qacc + v3 * s
            p_ref[x] = pacc
            q_ref[x] = qacc
            return carry

        lax.fori_loop(0, SUB, stage_c, 0)

        window_a = (depth >= za) & (depth < za + SUB)
        window_b = (depth >= zb) & (depth < zb + SUB)
        back_a = za % lanes
        back_b = (zb + lanes - group) % lanes
        live_b = first + 1 < count_ref[0]

        def stage_d(x, carry):
            pacc = p_ref[x]
            qacc = q_ref[x]
            for f in range(NF):
                lt, _ = laplace(t_ref, f, x)
                v3 = v3_ref[f, x]
                v2 = v3 - OMEGA * (v3 + lt)
                pacc = pacc + v2 * img1_ref[f, x]
                qacc = qacc + v2 * s1_ref[f, x]
            res = -OMEGA * jnp.where(upper, qacc - swap(qacc), pacc + swap(pacc))
            total_ref[xa + x, pl.ds(ya, SUB), :] += jnp.where(window_a, pltpu.roll(res, back_a, 1), 0.0)

            @pl.when(live_b)
            def _():
                total_ref[xb + x, pl.ds(yb, SUB), :] += jnp.where(window_b, pltpu.roll(res, back_b, 1), 0.0)

            return carry

        lax.fori_loop(0, SUB, stage_d, 0)


def subzone_pass(extended, spots, count):
    lanes = extended.shape[-1]
    home = spots.shape[0]
    ex, ey = extended.shape[1], extended.shape[2]

    def block_map(offset):
        def index(s, spots_ref, count_ref):
            live = jnp.minimum(2 * s + offset, jnp.maximum(count_ref[0] - 1, 0))
            return (0, spots_ref[live, 0], pl.multiple_of(spots_ref[live, 1], HALO), 0)
        return index

    f32 = jnp.float32
    padded = (NF, SUB + 2, SUB + 2 * PADY, lanes)
    block = (pl.Element(NF + 1), pl.Element(SUB), pl.Element(SUB), pl.Element(lanes))
    grid_spec = pltpu.PrefetchScalarGridSpec(
        num_scalar_prefetch=2,
        grid=((home + 1) // 2,),
        in_specs=[pl.BlockSpec(block, block_map(0)), pl.BlockSpec(block, block_map(1))],
        out_specs=pl.BlockSpec((ex, ey, lanes), lambda s, spots_ref, count_ref: (0, 0, 0)),
        scratch_shapes=[
            pltpu.VMEM((NF, SUB, SUB, lanes), f32),
            pltpu.VMEM((SUB, SUB, lanes), f32),
            pltpu.VMEM((SUB, SUB, lanes), f32),
            pltpu.VMEM(padded, f32),
            pltpu.VMEM(padded, f32),
            pltpu.VMEM(padded, f32),
            pltpu.VMEM((NF, SUB, SUB, lanes), f32),
            pltpu.VMEM((NF, SUB, SUB, lanes), f32),
            pltpu.VMEM((NF, SUB, SUB, lanes), f32),
            pltpu.VMEM((SUB, SUB, lanes), f32),
            pltpu.VMEM((SUB, SUB, lanes), f32),
        ],
    )
    return pl.pallas_call(
        subzone_kernel,
        grid_spec=grid_spec,
        out_shape=jax.ShapeDtypeStruct((ex, ey, lanes), f32),
        compiler_params=pltpu.CompilerParams(
            dimension_semantics=("arbitrary",), vmem_limit_bytes=100 * 1024 * 1024
        ),
    )(spots, count, extended, extended)


def shards(fields, modulus, anchors, home_count):
    data = jnp.concatenate([fields, modulus[None]], axis=0)
    extended = with_halo(data, (("vx", 1), ("vy", 2)), HALO)
    home = anchors.shape[2]
    spots = (anchors[0, 0] * HALO).astype(jnp.int32)
    count = home_count[0, 0].astype(jnp.int32)
    slots = jnp.arange(home, dtype=jnp.int32)
    live = slots < count
    edge = ((spots[:, 0] < HALO) | (spots[:, 0] + SUB > TX + HALO)) & live
    order = jnp.argsort(jnp.where(edge, 0, jnp.where(live, 1, 2)).astype(jnp.int32), stable=True)
    spots = spots[order]
    n_edge = jnp.sum(edge.astype(jnp.int32))
    n_edge = jnp.minimum(n_edge + n_edge % 2, count)
    rest = jnp.take(spots, (slots + n_edge) % home, axis=0)
    total = subzone_pass(extended, spots, n_edge[None])
    inner = subzone_pass(extended, rest, (count - n_edge)[None])
    from_above = passed_along(total[:HALO], "vx", -1)
    from_below = passed_along(total[TX + HALO :], "vx", 1)
    middle = total[HALO : HALO + TX] + inner[HALO : HALO + TX]
    middle = middle.at[:HALO].add(from_below).at[TX - HALO :].add(from_above)
    from_right = passed_along(middle[:, :HALO], "vy", -1)
    from_left = passed_along(middle[:, TY + HALO :], "vy", 1)
    owned = middle[:, HALO : HALO + TY]
    owned = owned.at[:, :HALO].add(from_left).at[:, TY - HALO :].add(from_right)
    return owned


def solution(mesh):
    return jax.shard_map(
        shards,
        mesh=mesh,
        in_specs=(
            P(None, "vx", "vy", None),
            P("vx", "vy", None),
            P("vx", "vy", None, None),
            P("vx", "vy"),
        ),
        out_specs=P("vx", "vy", None),
        check_vma=False,
    )
```

```python
import functools

import jax
import jax.numpy as jnp
from jax import lax
from jax.experimental import pallas as pl
from jax.experimental.pallas import tpu as pltpu
from jax.sharding import PartitionSpec as P

NF = 4
SUB = 32
HALO = 16
TX = 64
TY = 160
RFWD = 3


OMEGA = 0.07
PADY = 8
STEP_FLOPS = 30_000_000_000
STEP_BYTES = 2 * (NF + 1) * SUB * SUB * 128 * 2


def with_halo(x, sides, width):
    for axis, dim in sides:
        size, length = (lax.axis_size(axis), x.shape[dim])
        up = [(i, (i + 1) % size) for i in range(size - 1)]
        down = [(j, i) for i, j in up]
        last = lax.slice_in_dim(x, length - width, length, axis=dim)
        first = lax.slice_in_dim(x, 0, width, axis=dim)
        before = lax.ppermute(last, axis, up)
        after = lax.ppermute(first, axis, down)
        x = jnp.concatenate([before, x, after], axis=dim)
    return x


def passed_along(x, axis, by):
    length = lax.axis_size(axis)
    pairs = [(i, i + by) for i in range(length) if 0 <= i + by < length]
    return lax.ppermute(x, axis, pairs)


def subzone_kernel(spots_ref, count_ref, block_a, mod_a, block_b, mod_b, total_ref,
                   um_ref, mur_ref, muis_ref, w1_ref, w2_ref, t_ref,
                   img1_ref, s1_ref, v3_ref, p_ref, q_ref):
    step = pl.program_id(0)
    lanes = block_a.shape[-1]
    half = lanes // 2
    group = half // 2
    first = 2 * step
    second = jnp.minimum(first + 1, count_ref[0] - 1)

    @pl.when(step == 0)
    def _():
        total_ref[...] = jnp.zeros_like(total_ref)
        w1_ref[...] = jnp.zeros_like(w1_ref)
        w2_ref[...] = jnp.zeros_like(w2_ref)
        t_ref[...] = jnp.zeros_like(t_ref)

    @pl.when(first < count_ref[0])
    def _():
        xa = spots_ref[first, 0]
        ya = pl.multiple_of(spots_ref[first, 1], HALO)
        za = spots_ref[first, 2]
        xb = spots_ref[second, 0]
        yb = pl.multiple_of(spots_ref[second, 1], HALO)
        zb = spots_ref[second, 2]
        lane = lax.broadcasted_iota(jnp.int32, (SUB, lanes), 1)
        depth = lane % half
        in_a = (lane % half) < group
        upper = lane >= half
        not_low = (lane % group) != 0
        not_high = (lane % group) != group - 1
        shift_a = (lanes - za) % lanes
        shift_b = (group - zb + lanes) % lanes

        def swap(v):
            return pltpu.roll(v, half, 1)

        def packed(ref_a, ref_b, k, x):
            a = ref_a[k, x].astype(jnp.float32)
            b = ref_b[k, x].astype(jnp.float32)
            return jnp.where(in_a, pltpu.roll(a, shift_a, 1), pltpu.roll(b, shift_b, 1))

        def laplace(ref, f, x):
            c = ref[f, x + 1, PADY:PADY + SUB, :]
            side = ref[f, x, PADY:PADY + SUB, :] + ref[f, x + 2, PADY:PADY + SUB, :]
            side = side + ref[f, x + 1, PADY - 1:PADY - 1 + SUB, :]
            side = side + ref[f, x + 1, PADY + 1:PADY + 1 + SUB, :]
            side = side + jnp.where(not_low, pltpu.roll(c, 1, 1), 0.0)
            side = side + jnp.where(not_high, pltpu.roll(c, lanes - 1, 1), 0.0)
            return 6.0 * c - side, c

        def stage_a(x, carry):
            mu = packed(mod_a, mod_b, 0, x)
            smu = swap(mu)
            mur_ref[x] = jnp.where(upper, smu, mu)
            muis_ref[x] = jnp.where(upper, mu, -smu)
            for f in range(NF):
                u = packed(block_a, block_b, f, x)
                um_ref[f, x] = u
                w1_ref[f, x + 1, PADY:PADY + SUB, :] = OMEGA * u
            return carry

        lax.fori_loop(0, SUB, stage_a, 0)

        def stage_b(x, carry):
            mur = mur_ref[x]
            muis = muis_ref[x]
            for f in range(NF):
                img, c = laplace(w1_ref, f, x)
                s = swap(img)
                u = um_ref[f, x]
                w2_ref[f, x + 1, PADY:PADY + SUB, :] = c + OMEGA * (u - c - (mur * img + muis * s))
                img1_ref[f, x] = img
                s1_ref[f, x] = s
            return carry

        lax.fori_loop(0, SUB, stage_b, 0)

        def stage_c(x, carry):
            mur = mur_ref[x]
            muis = muis_ref[x]
            pacc = jnp.zeros((SUB, lanes), jnp.float32)
            qacc = jnp.zeros((SUB, lanes), jnp.float32)
            for f in range(NF):
                img, c = laplace(w2_ref, f, x)
                s = swap(img)
                u = um_ref[f, x]
                w3 = c + OMEGA * (u - c - (mur * img + muis * s))
                v3 = w3 - u
                t_ref[f, x + 1, PADY:PADY + SUB, :] = mur * v3 - muis * swap(v3)
                v3_ref[f, x] = v3
                pacc = pacc + v3 * img
                qacc = qacc + v3 * s
            p_ref[x] = pacc
            q_ref[x] = qacc
            return carry

        lax.fori_loop(0, SUB, stage_c, 0)

        window_a = (depth >= za) & (depth < za + SUB)
        window_b = (depth >= zb) & (depth < zb + SUB)
        back_a = za % lanes
        back_b = (zb + lanes - group) % lanes
        live_b = first + 1 < count_ref[0]

        def stage_d(x, carry):
            pacc = p_ref[x]
            qacc = q_ref[x]
            for f in range(NF):
                lt, _ = laplace(t_ref, f, x)
                v3 = v3_ref[f, x]
                v2 = v3 - OMEGA * (v3 + lt)
                pacc = pacc + v2 * img1_ref[f, x]
                qacc = qacc + v2 * s1_ref[f, x]
            res = -OMEGA * jnp.where(upper, qacc - swap(qacc), pacc + swap(pacc))
            total_ref[xa + x, pl.ds(ya, SUB), :] += jnp.where(window_a, pltpu.roll(res, back_a, 1), 0.0)

            @pl.when(live_b)
            def _():
                total_ref[xb + x, pl.ds(yb, SUB), :] += jnp.where(window_b, pltpu.roll(res, back_b, 1), 0.0)

            return carry

        lax.fori_loop(0, SUB, stage_d, 0)


def subzone_pass(fields, modulus, spots, count, shift, extent):
    lanes = fields.shape[-1]
    home = spots.shape[0]
    ex, ey = extent

    def block_map(offset, base):
        def index(s, spots_ref, count_ref):
            live = jnp.minimum(2 * s + offset, jnp.maximum(count_ref[0] - 1, 0))
            row = jnp.clip(spots_ref[live, 0] - shift, 0, fields.shape[1] - SUB)
            col = jnp.clip(spots_ref[live, 1] - shift, 0, fields.shape[2] - SUB)
            col = pl.multiple_of(col, HALO)
            return (base, row, col, 0)
        return index

    f32 = jnp.float32
    padded = (NF, SUB + 2, SUB + 2 * PADY, lanes)
    block = (pl.Element(NF), pl.Element(SUB), pl.Element(SUB), pl.Element(lanes))
    mod_block = (pl.Element(1), pl.Element(SUB), pl.Element(SUB), pl.Element(lanes))
    base = modulus.shape[0] - 1
    grid_spec = pltpu.PrefetchScalarGridSpec(
        num_scalar_prefetch=2,
        grid=((home + 1) // 2,),
        in_specs=[
            pl.BlockSpec(block, block_map(0, 0)),
            pl.BlockSpec(mod_block, block_map(0, base)),
            pl.BlockSpec(block, block_map(1, 0)),
            pl.BlockSpec(mod_block, block_map(1, base)),
        ],
        out_specs=pl.BlockSpec((ex, ey, lanes), lambda s, spots_ref, count_ref: (0, 0, 0)),
        scratch_shapes=[
            pltpu.VMEM((NF, SUB, SUB, lanes), f32),
            pltpu.VMEM((SUB, SUB, lanes), f32),
            pltpu.VMEM((SUB, SUB, lanes), f32),
            pltpu.VMEM(padded, f32),
            pltpu.VMEM(padded, f32),
            pltpu.VMEM(padded, f32),
            pltpu.VMEM((NF, SUB, SUB, lanes), f32),
            pltpu.VMEM((NF, SUB, SUB, lanes), f32),
            pltpu.VMEM((NF, SUB, SUB, lanes), f32),
            pltpu.VMEM((SUB, SUB, lanes), f32),
            pltpu.VMEM((SUB, SUB, lanes), f32),
        ],
    )
    return pl.pallas_call(
        subzone_kernel,
        grid_spec=grid_spec,
        out_shape=jax.ShapeDtypeStruct((ex, ey, lanes), f32),
        cost_estimate=pl.CostEstimate(
            flops=STEP_FLOPS * ((home + 1) // 2), transcendentals=0, bytes_accessed=STEP_BYTES * ((home + 1) // 2)
        ),
        compiler_params=pltpu.CompilerParams(
            dimension_semantics=("arbitrary",), vmem_limit_bytes=100 * 1024 * 1024
        ),
    )(spots, count, fields, modulus, fields, modulus)


def shards(fields, modulus, anchors, home_count):
    home = anchors.shape[2]
    extent = (TX + 2 * HALO, TY + 2 * HALO)
    spots = (anchors[0, 0] * HALO).astype(jnp.int32)
    count = home_count[0, 0].astype(jnp.int32)
    slots = jnp.arange(home, dtype=jnp.int32)
    live = slots < count
    edge = ((spots[:, 0] < HALO) | (spots[:, 0] + SUB > TX + HALO)) & live
    side = (spots[:, 1] < HALO) | (spots[:, 1] + SUB > TY + HALO)
    inner = live & ~edge & ~side
    key = jnp.where(inner, 0, jnp.where(edge, 1, jnp.where(live, 2, 3)))
    order = jnp.argsort(key.astype(jnp.int32), stable=True)
    spots = spots[order]
    n_inner = jnp.sum(inner.astype(jnp.int32))
    n_edge = jnp.sum(edge.astype(jnp.int32))
    first = (n_inner // 2) * 2
    second = n_edge + n_inner % 2
    second = jnp.minimum(second + second % 2, count - first)
    middle_spots = jnp.take(spots, (slots + first) % home, axis=0)
    rest = jnp.take(spots, (slots + first + second) % home, axis=0)
    early = subzone_pass(fields, modulus[None], spots, first[None], HALO, extent)
    data = jnp.concatenate([fields, modulus[None]], axis=0)
    extended = with_halo(data, (("vy", 2), ("vx", 1)), HALO)
    total = subzone_pass(extended, extended, middle_spots, second[None], 0, extent)
    late = subzone_pass(extended, extended, rest, (count - first - second)[None], 0, extent)
    from_above = passed_along(total[:HALO], "vx", -1)
    from_below = passed_along(total[TX + HALO :], "vx", 1)
    middle = total[HALO : HALO + TX] + late[HALO : HALO + TX] + early[HALO : HALO + TX]
    middle = middle.at[:HALO].add(from_below).at[TX - HALO :].add(from_above)
    from_right = passed_along(middle[:, :HALO], "vy", -1)
    from_left = passed_along(middle[:, TY + HALO :], "vy", 1)
    owned = middle[:, HALO : HALO + TY]
    owned = owned.at[:, :HALO].add(from_left).at[:, TY - HALO :].add(from_right)
    return owned


def solution(mesh):
    return jax.shard_map(
        shards,
        mesh=mesh,
        in_specs=(
            P(None, "vx", "vy", None),
            P("vx", "vy", None),
            P("vx", "vy", None, None),
            P("vx", "vy"),
        ),
        out_specs=P("vx", "vy", None),
        check_vma=False,
    )
```

```python
import functools

import jax
import jax.numpy as jnp
from jax import lax
from jax.experimental import pallas as pl
from jax.experimental.pallas import tpu as pltpu
from jax.sharding import PartitionSpec as P

NF = 4
SUB = 32
HALO = 16
TX = 64
TY = 160
RFWD = 3


OMEGA = 0.07
PADY = 8
EARLY = 6
STEP_FLOPS = 30_000_000_000
STEP_BYTES = 2 * (NF + 1) * SUB * SUB * 128 * 2


def with_halo(x, sides, width):
    for axis, dim in sides:
        size, length = (lax.axis_size(axis), x.shape[dim])
        up = [(i, (i + 1) % size) for i in range(size - 1)]
        down = [(j, i) for i, j in up]
        last = lax.slice_in_dim(x, length - width, length, axis=dim)
        first = lax.slice_in_dim(x, 0, width, axis=dim)
        before = lax.ppermute(last, axis, up)
        after = lax.ppermute(first, axis, down)
        x = jnp.concatenate([before, x, after], axis=dim)
    return x


def passed_along(x, axis, by):
    length = lax.axis_size(axis)
    pairs = [(i, i + by) for i in range(length) if 0 <= i + by < length]
    return lax.ppermute(x, axis, pairs)


def subzone_kernel(spots_ref, count_ref, block_a, mod_a, block_b, mod_b, total_ref,
                   um_ref, mur_ref, muis_ref, w1_ref, w2_ref, t_ref,
                   img1_ref, s1_ref, v3_ref, p_ref, q_ref):
    step = pl.program_id(0)
    lanes = block_a.shape[-1]
    half = lanes // 2
    group = half // 2
    first = 2 * step
    second = jnp.minimum(first + 1, count_ref[0] - 1)

    @pl.when(step == 0)
    def _():
        total_ref[...] = jnp.zeros_like(total_ref)
        w1_ref[...] = jnp.zeros_like(w1_ref)
        w2_ref[...] = jnp.zeros_like(w2_ref)
        t_ref[...] = jnp.zeros_like(t_ref)

    @pl.when(first < count_ref[0])
    def _():
        xa = spots_ref[first, 0]
        ya = pl.multiple_of(spots_ref[first, 1], HALO)
        za = spots_ref[first, 2]
        xb = spots_ref[second, 0]
        yb = pl.multiple_of(spots_ref[second, 1], HALO)
        zb = spots_ref[second, 2]
        lane = lax.broadcasted_iota(jnp.int32, (SUB, lanes), 1)
        depth = lane % half
        in_a = (lane % half) < group
        upper = lane >= half
        not_low = (lane % group) != 0
        not_high = (lane % group) != group - 1
        shift_a = (lanes - za) % lanes
        shift_b = (group - zb + lanes) % lanes

        def swap(v):
            return pltpu.roll(v, half, 1)

        def packed(ref_a, ref_b, k, x):
            a = ref_a[k, x].astype(jnp.float32)
            b = ref_b[k, x].astype(jnp.float32)
            return jnp.where(in_a, pltpu.roll(a, shift_a, 1), pltpu.roll(b, shift_b, 1))

        def laplace(ref, f, x):
            c = ref[f, x + 1, PADY:PADY + SUB, :]
            side = ref[f, x, PADY:PADY + SUB, :] + ref[f, x + 2, PADY:PADY + SUB, :]
            side = side + ref[f, x + 1, PADY - 1:PADY - 1 + SUB, :]
            side = side + ref[f, x + 1, PADY + 1:PADY + 1 + SUB, :]
            side = side + jnp.where(not_low, pltpu.roll(c, 1, 1), 0.0)
            side = side + jnp.where(not_high, pltpu.roll(c, lanes - 1, 1), 0.0)
            return 6.0 * c - side, c

        def stage_a(x, carry):
            mu = packed(mod_a, mod_b, 0, x)
            smu = swap(mu)
            mur_ref[x] = jnp.where(upper, smu, mu)
            muis_ref[x] = jnp.where(upper, mu, -smu)
            for f in range(NF):
                u = packed(block_a, block_b, f, x)
                um_ref[f, x] = u
                w1_ref[f, x + 1, PADY:PADY + SUB, :] = OMEGA * u
            return carry

        lax.fori_loop(0, SUB, stage_a, 0)

        def stage_b(x, carry):
            mur = mur_ref[x]
            muis = muis_ref[x]
            for f in range(NF):
                img, c = laplace(w1_ref, f, x)
                s = swap(img)
                u = um_ref[f, x]
                w2_ref[f, x + 1, PADY:PADY + SUB, :] = c + OMEGA * (u - c - (mur * img + muis * s))
                img1_ref[f, x] = img
                s1_ref[f, x] = s
            return carry

        lax.fori_loop(0, SUB, stage_b, 0)

        def stage_c(x, carry):
            mur = mur_ref[x]
            muis = muis_ref[x]
            pacc = jnp.zeros((SUB, lanes), jnp.float32)
            qacc = jnp.zeros((SUB, lanes), jnp.float32)
            for f in range(NF):
                img, c = laplace(w2_ref, f, x)
                s = swap(img)
                u = um_ref[f, x]
                w3 = c + OMEGA * (u - c - (mur * img + muis * s))
                v3 = w3 - u
                t_ref[f, x + 1, PADY:PADY + SUB, :] = mur * v3 - muis * swap(v3)
                v3_ref[f, x] = v3
                pacc = pacc + v3 * img
                qacc = qacc + v3 * s
            p_ref[x] = pacc
            q_ref[x] = qacc
            return carry

        lax.fori_loop(0, SUB, stage_c, 0)

        window_a = (depth >= za) & (depth < za + SUB)
        window_b = (depth >= zb) & (depth < zb + SUB)
        back_a = za % lanes
        back_b = (zb + lanes - group) % lanes
        live_b = first + 1 < count_ref[0]

        def stage_d(x, carry):
            pacc = p_ref[x]
            qacc = q_ref[x]
            for f in range(NF):
                lt, _ = laplace(t_ref, f, x)
                v3 = v3_ref[f, x]
                v2 = v3 - OMEGA * (v3 + lt)
                pacc = pacc + v2 * img1_ref[f, x]
                qacc = qacc + v2 * s1_ref[f, x]
            res = -OMEGA * jnp.where(upper, qacc - swap(qacc), pacc + swap(pacc))
            total_ref[xa + x, pl.ds(ya, SUB), :] += jnp.where(window_a, pltpu.roll(res, back_a, 1), 0.0)

            @pl.when(live_b)
            def _():
                total_ref[xb + x, pl.ds(yb, SUB), :] += jnp.where(window_b, pltpu.roll(res, back_b, 1), 0.0)

            return carry

        lax.fori_loop(0, SUB, stage_d, 0)


def subzone_pass(fields, modulus, spots, count, shift, extent):
    lanes = fields.shape[-1]
    home = spots.shape[0]
    ex, ey = extent

    def block_map(offset, base):
        def index(s, spots_ref, count_ref):
            live = jnp.minimum(2 * s + offset, jnp.maximum(count_ref[0] - 1, 0))
            row = jnp.clip(spots_ref[live, 0] - shift[0], 0, fields.shape[1] - SUB)
            col = jnp.clip(spots_ref[live, 1] - shift[1], 0, fields.shape[2] - SUB)
            col = pl.multiple_of(col, HALO)
            return (base, row, col, 0)
        return index

    f32 = jnp.float32
    padded = (NF, SUB + 2, SUB + 2 * PADY, lanes)
    block = (pl.Element(NF), pl.Element(SUB), pl.Element(SUB), pl.Element(lanes))
    mod_block = (pl.Element(1), pl.Element(SUB), pl.Element(SUB), pl.Element(lanes))
    base = modulus.shape[0] - 1
    grid_spec = pltpu.PrefetchScalarGridSpec(
        num_scalar_prefetch=2,
        grid=((home + 1) // 2,),
        in_specs=[
            pl.BlockSpec(block, block_map(0, 0)),
            pl.BlockSpec(mod_block, block_map(0, base)),
            pl.BlockSpec(block, block_map(1, 0)),
            pl.BlockSpec(mod_block, block_map(1, base)),
        ],
        out_specs=pl.BlockSpec((ex, ey, lanes), lambda s, spots_ref, count_ref: (0, 0, 0)),
        scratch_shapes=[
            pltpu.VMEM((NF, SUB, SUB, lanes), f32),
            pltpu.VMEM((SUB, SUB, lanes), f32),
            pltpu.VMEM((SUB, SUB, lanes), f32),
            pltpu.VMEM(padded, f32),
            pltpu.VMEM(padded, f32),
            pltpu.VMEM(padded, f32),
            pltpu.VMEM((NF, SUB, SUB, lanes), f32),
            pltpu.VMEM((NF, SUB, SUB, lanes), f32),
            pltpu.VMEM((NF, SUB, SUB, lanes), f32),
            pltpu.VMEM((SUB, SUB, lanes), f32),
            pltpu.VMEM((SUB, SUB, lanes), f32),
        ],
    )
    return pl.pallas_call(
        subzone_kernel,
        grid_spec=grid_spec,
        out_shape=jax.ShapeDtypeStruct((ex, ey, lanes), f32),
        cost_estimate=pl.CostEstimate(
            flops=STEP_FLOPS * ((home + 1) // 2), transcendentals=0, bytes_accessed=STEP_BYTES * ((home + 1) // 2)
        ),
        compiler_params=pltpu.CompilerParams(
            dimension_semantics=("arbitrary",), vmem_limit_bytes=100 * 1024 * 1024
        ),
    )(spots, count, fields, modulus, fields, modulus)


def shards(fields, modulus, anchors, home_count):
    home = anchors.shape[2]
    extent = (TX + 2 * HALO, TY + 2 * HALO)
    spots = (anchors[0, 0] * HALO).astype(jnp.int32)
    count = home_count[0, 0].astype(jnp.int32)
    slots = jnp.arange(home, dtype=jnp.int32)
    live = slots < count
    edge = ((spots[:, 0] < HALO) | (spots[:, 0] + SUB > TX + HALO)) & live
    inner = live & ~edge
    n_inner = jnp.sum(inner.astype(jnp.int32))
    n_edge = jnp.sum(edge.astype(jnp.int32))
    first = jnp.minimum(EARLY, (n_inner // 2) * 2)
    rank = jnp.cumsum(inner.astype(jnp.int32)) - 1
    key = jnp.where(inner & (rank < first), 0, jnp.where(edge, 1, jnp.where(live, 2, 3)))
    order = jnp.argsort(key.astype(jnp.int32), stable=True)
    spots = spots[order]
    second = jnp.minimum(n_edge + n_edge % 2, count - first)
    middle_spots = jnp.take(spots, (slots + first) % home, axis=0)
    rest = jnp.take(spots, (slots + first + second) % home, axis=0)
    data = jnp.concatenate([fields, modulus[None]], axis=0)
    wide = with_halo(data, (("vy", 2),), HALO)
    early = subzone_pass(wide, wide, spots, first[None], (HALO, 0), extent)
    extended = with_halo(wide, (("vx", 1),), HALO)
    total = subzone_pass(extended, extended, middle_spots, second[None], (0, 0), extent)
    late = subzone_pass(extended, extended, rest, (count - first - second)[None], (0, 0), extent)
    from_above = passed_along(total[:HALO], "vx", -1)
    from_below = passed_along(total[TX + HALO :], "vx", 1)
    middle = total[HALO : HALO + TX] + late[HALO : HALO + TX] + early[HALO : HALO + TX]
    middle = middle.at[:HALO].add(from_below).at[TX - HALO :].add(from_above)
    from_right = passed_along(middle[:, :HALO], "vy", -1)
    from_left = passed_along(middle[:, TY + HALO :], "vy", 1)
    owned = middle[:, HALO : HALO + TY]
    owned = owned.at[:, :HALO].add(from_left).at[:, TY - HALO :].add(from_right)
    return owned


def solution(mesh):
    return jax.shard_map(
        shards,
        mesh=mesh,
        in_specs=(
            P(None, "vx", "vy", None),
            P("vx", "vy", None),
            P("vx", "vy", None, None),
            P("vx", "vy"),
        ),
        out_specs=P("vx", "vy", None),
        check_vma=False,
    )
```

```python
import functools

import jax
import jax.numpy as jnp
from jax import lax
from jax.experimental import pallas as pl
from jax.experimental.pallas import tpu as pltpu
from jax.sharding import PartitionSpec as P

NF = 4
SUB = 32
HALO = 16
TX = 64
TY = 160
RFWD = 3


OMEGA = 0.07
PADY = 8
STEP_FLOPS = 30_000_000_000
STEP_BYTES = 2 * (NF + 1) * SUB * SUB * 128 * 2


def with_halo(x, sides, width):
    for axis, dim in sides:
        size, length = (lax.axis_size(axis), x.shape[dim])
        up = [(i, (i + 1) % size) for i in range(size - 1)]
        down = [(j, i) for i, j in up]
        last = lax.slice_in_dim(x, length - width, length, axis=dim)
        first = lax.slice_in_dim(x, 0, width, axis=dim)
        before = lax.ppermute(last, axis, up)
        after = lax.ppermute(first, axis, down)
        x = jnp.concatenate([before, x, after], axis=dim)
    return x


def passed_along(x, axis, by):
    length = lax.axis_size(axis)
    pairs = [(i, i + by) for i in range(length) if 0 <= i + by < length]
    return lax.ppermute(x, axis, pairs)


def subzone_kernel(spots_ref, count_ref, block_a, mod_a, block_b, mod_b, total_ref,
                   um_ref, mur_ref, muis_ref, w1_ref, w2_ref, t_ref,
                   img1_ref, s1_ref, v3_ref, p_ref, q_ref):
    step = pl.program_id(0)
    lanes = block_a.shape[-1]
    half = lanes // 2
    group = half // 2
    first = 2 * step
    second = jnp.minimum(first + 1, count_ref[0] - 1)

    @pl.when(step == 0)
    def _():
        total_ref[...] = jnp.zeros_like(total_ref)
        w1_ref[...] = jnp.zeros_like(w1_ref)
        w2_ref[...] = jnp.zeros_like(w2_ref)
        t_ref[...] = jnp.zeros_like(t_ref)

    @pl.when(first < count_ref[0])
    def _():
        xa = spots_ref[first, 0]
        ya = pl.multiple_of(spots_ref[first, 1], HALO)
        za = spots_ref[first, 2]
        xb = spots_ref[second, 0]
        yb = pl.multiple_of(spots_ref[second, 1], HALO)
        zb = spots_ref[second, 2]
        lane = lax.broadcasted_iota(jnp.int32, (SUB, lanes), 1)
        depth = lane % half
        in_a = (lane % half) < group
        upper = lane >= half
        not_low = (lane % group) != 0
        not_high = (lane % group) != group - 1
        shift_a = (lanes - za) % lanes
        shift_b = (group - zb + lanes) % lanes

        def swap(v):
            return pltpu.roll(v, half, 1)

        def packed(ref_a, ref_b, k, x):
            a = ref_a[k, x].astype(jnp.float32)
            b = ref_b[k, x].astype(jnp.float32)
            return jnp.where(in_a, pltpu.roll(a, shift_a, 1), pltpu.roll(b, shift_b, 1))

        def laplace(ref, f, x):
            c = ref[f, x + 1, PADY:PADY + SUB, :]
            side = ref[f, x, PADY:PADY + SUB, :] + ref[f, x + 2, PADY:PADY + SUB, :]
            side = side + ref[f, x + 1, PADY - 1:PADY - 1 + SUB, :]
            side = side + ref[f, x + 1, PADY + 1:PADY + 1 + SUB, :]
            side = side + jnp.where(not_low, pltpu.roll(c, 1, 1), 0.0)
            side = side + jnp.where(not_high, pltpu.roll(c, lanes - 1, 1), 0.0)
            return 6.0 * c - side, c

        def stage_a(x, carry):
            mu = packed(mod_a, mod_b, 0, x)
            smu = swap(mu)
            mur_ref[x] = jnp.where(upper, smu, mu)
            muis_ref[x] = jnp.where(upper, mu, -smu)
            for f in range(NF):
                u = packed(block_a, block_b, f, x)
                um_ref[f, x] = u
                w1_ref[f, x + 1, PADY:PADY + SUB, :] = OMEGA * u
            return carry

        lax.fori_loop(0, SUB, stage_a, 0)

        def stage_b(x, carry):
            mur = mur_ref[x]
            muis = muis_ref[x]
            for f in range(NF):
                img, c = laplace(w1_ref, f, x)
                s = swap(img)
                u = um_ref[f, x]
                w2_ref[f, x + 1, PADY:PADY + SUB, :] = c + OMEGA * (u - c - (mur * img + muis * s))
                img1_ref[f, x] = img
                s1_ref[f, x] = s
            return carry

        lax.fori_loop(0, SUB, stage_b, 0)

        def stage_c(x, carry):
            mur = mur_ref[x]
            muis = muis_ref[x]
            pacc = jnp.zeros((SUB, lanes), jnp.float32)
            qacc = jnp.zeros((SUB, lanes), jnp.float32)
            for f in range(NF):
                img, c = laplace(w2_ref, f, x)
                s = swap(img)
                u = um_ref[f, x]
                w3 = c + OMEGA * (u - c - (mur * img + muis * s))
                v3 = w3 - u
                t_ref[f, x + 1, PADY:PADY + SUB, :] = mur * v3 - muis * swap(v3)
                v3_ref[f, x] = v3
                pacc = pacc + v3 * img
                qacc = qacc + v3 * s
            p_ref[x] = pacc
            q_ref[x] = qacc
            return carry

        lax.fori_loop(0, SUB, stage_c, 0)

        window_a = (depth >= za) & (depth < za + SUB)
        window_b = (depth >= zb) & (depth < zb + SUB)
        back_a = za % lanes
        back_b = (zb + lanes - group) % lanes
        live_b = first + 1 < count_ref[0]

        def stage_d(x, carry):
            pacc = p_ref[x]
            qacc = q_ref[x]
            for f in range(NF):
                lt, _ = laplace(t_ref, f, x)
                v3 = v3_ref[f, x]
                v2 = v3 - OMEGA * (v3 + lt)
                pacc = pacc + v2 * img1_ref[f, x]
                qacc = qacc + v2 * s1_ref[f, x]
            res = -OMEGA * jnp.where(upper, qacc - swap(qacc), pacc + swap(pacc))
            total_ref[xa + x, pl.ds(ya, SUB), :] += jnp.where(window_a, pltpu.roll(res, back_a, 1), 0.0)

            @pl.when(live_b)
            def _():
                total_ref[xb + x, pl.ds(yb, SUB), :] += jnp.where(window_b, pltpu.roll(res, back_b, 1), 0.0)

            return carry

        lax.fori_loop(0, SUB, stage_d, 0)


def subzone_pass(fields, modulus, spots, count, shift, extent):
    lanes = fields.shape[-1]
    home = spots.shape[0]
    ex, ey = extent

    def block_map(offset, base):
        def index(s, spots_ref, count_ref):
            live = jnp.minimum(2 * s + offset, jnp.maximum(count_ref[0] - 1, 0))
            row = jnp.clip(spots_ref[live, 0] - shift, 0, fields.shape[1] - SUB)
            col = jnp.clip(spots_ref[live, 1] - shift, 0, fields.shape[2] - SUB)
            col = pl.multiple_of(col, HALO)
            return (base, row, col, 0)
        return index

    f32 = jnp.float32
    padded = (NF, SUB + 2, SUB + 2 * PADY, lanes)
    block = (pl.Element(NF), pl.Element(SUB), pl.Element(SUB), pl.Element(lanes))
    mod_block = (pl.Element(1), pl.Element(SUB), pl.Element(SUB), pl.Element(lanes))
    base = modulus.shape[0] - 1
    grid_spec = pltpu.PrefetchScalarGridSpec(
        num_scalar_prefetch=2,
        grid=((home + 1) // 2,),
        in_specs=[
            pl.BlockSpec(block, block_map(0, 0)),
            pl.BlockSpec(mod_block, block_map(0, base)),
            pl.BlockSpec(block, block_map(1, 0)),
            pl.BlockSpec(mod_block, block_map(1, base)),
        ],
        out_specs=pl.BlockSpec((ex, ey, lanes), lambda s, spots_ref, count_ref: (0, 0, 0)),
        scratch_shapes=[
            pltpu.VMEM((NF, SUB, SUB, lanes), f32),
            pltpu.VMEM((SUB, SUB, lanes), f32),
            pltpu.VMEM((SUB, SUB, lanes), f32),
            pltpu.VMEM(padded, f32),
            pltpu.VMEM(padded, f32),
            pltpu.VMEM(padded, f32),
            pltpu.VMEM((NF, SUB, SUB, lanes), f32),
            pltpu.VMEM((NF, SUB, SUB, lanes), f32),
            pltpu.VMEM((NF, SUB, SUB, lanes), f32),
            pltpu.VMEM((SUB, SUB, lanes), f32),
            pltpu.VMEM((SUB, SUB, lanes), f32),
        ],
    )
    return pl.pallas_call(
        subzone_kernel,
        grid_spec=grid_spec,
        out_shape=jax.ShapeDtypeStruct((ex, ey, lanes), f32),
        cost_estimate=pl.CostEstimate(
            flops=STEP_FLOPS * ((home + 1) // 2), transcendentals=0, bytes_accessed=STEP_BYTES * ((home + 1) // 2)
        ),
        compiler_params=pltpu.CompilerParams(
            dimension_semantics=("arbitrary",), vmem_limit_bytes=100 * 1024 * 1024
        ),
    )(spots, count, fields, modulus, fields, modulus)


def shards(fields, modulus, anchors, home_count):
    home = anchors.shape[2]
    extent = (TX + 2 * HALO, TY + 2 * HALO)
    spots = (anchors[0, 0] * HALO).astype(jnp.int32)
    count = home_count[0, 0].astype(jnp.int32)
    slots = jnp.arange(home, dtype=jnp.int32)
    live = slots < count
    edge = ((spots[:, 0] < HALO) | (spots[:, 0] + SUB > TX + HALO)) & live
    side = (spots[:, 1] < HALO) | (spots[:, 1] + SUB > TY + HALO)
    inner = live & ~edge & ~side
    key = jnp.where(inner, 0, jnp.where(edge, 1, jnp.where(live, 2, 3)))
    order = jnp.argsort(key.astype(jnp.int32), stable=True)
    spots = spots[order]
    n_inner = jnp.sum(inner.astype(jnp.int32))
    n_edge = jnp.sum(edge.astype(jnp.int32))
    first = (n_inner // 2) * 2
    second = n_edge + n_inner % 2
    second = jnp.minimum(second + second % 2, count - first)
    middle_spots = jnp.take(spots, (slots + first) % home, axis=0)
    rest = jnp.take(spots, (slots + first + second) % home, axis=0)
    lead = jnp.minimum(first, 2)
    follow = jnp.take(spots, (slots + lead) % home, axis=0)
    early = subzone_pass(fields, modulus[None], spots, lead[None], HALO, extent)
    early = early + subzone_pass(fields, modulus[None], follow, (first - lead)[None], HALO, extent)
    data = jnp.concatenate([fields, modulus[None]], axis=0)
    extended = with_halo(data, (("vy", 2), ("vx", 1)), HALO)
    total = subzone_pass(extended, extended, middle_spots, second[None], 0, extent)
    late = subzone_pass(extended, extended, rest, (count - first - second)[None], 0, extent)
    from_above = passed_along(total[:HALO], "vx", -1)
    from_below = passed_along(total[TX + HALO :], "vx", 1)
    middle = total[HALO : HALO + TX] + late[HALO : HALO + TX] + early[HALO : HALO + TX]
    middle = middle.at[:HALO].add(from_below).at[TX - HALO :].add(from_above)
    from_right = passed_along(middle[:, :HALO], "vy", -1)
    from_left = passed_along(middle[:, TY + HALO :], "vy", 1)
    owned = middle[:, HALO : HALO + TY]
    owned = owned.at[:, :HALO].add(from_left).at[:, TY - HALO :].add(from_right)
    return owned


def solution(mesh):
    return jax.shard_map(
        shards,
        mesh=mesh,
        in_specs=(
            P(None, "vx", "vy", None),
            P("vx", "vy", None),
            P("vx", "vy", None, None),
            P("vx", "vy"),
        ),
        out_specs=P("vx", "vy", None),
        check_vma=False,
    )
```

```python
import functools

import jax
import jax.numpy as jnp
from jax import lax
from jax.experimental import pallas as pl
from jax.experimental.pallas import tpu as pltpu
from jax.sharding import PartitionSpec as P

NF = 4
SUB = 32
HALO = 16
TX = 64
TY = 160
RFWD = 3


OMEGA = 0.07
PADY = 8
STEP_FLOPS = 30_000_000_000
STEP_BYTES = 2 * (NF + 1) * SUB * SUB * 128 * 2


def shifted(x, by_x, by_y):
    nx, ny = lax.axis_size("vx"), lax.axis_size("vy")
    pairs = []
    for a in range(nx):
        for b in range(ny):
            if 0 <= a + by_x < nx and 0 <= b + by_y < ny:
                pairs.append((a * ny + b, (a + by_x) * ny + b + by_y))
    return lax.ppermute(x, ("vx", "vy"), pairs)


def with_halo(x, width):
    rows, cols = x.shape[1], x.shape[2]
    top = x[:, rows - width :]
    bottom = x[:, :width]
    xlo = shifted(top, 1, 0)
    xhi = shifted(bottom, -1, 0)
    ylo = shifted(x[:, :, cols - width :], 0, 1)
    yhi = shifted(x[:, :, :width], 0, -1)
    c_ll = shifted(top[:, :, cols - width :], 1, 1)
    c_lh = shifted(top[:, :, :width], 1, -1)
    c_hl = shifted(bottom[:, :, cols - width :], -1, 1)
    c_hh = shifted(bottom[:, :, :width], -1, -1)
    left = jnp.concatenate([c_ll, ylo, c_hl], axis=1)
    right = jnp.concatenate([c_lh, yhi, c_hh], axis=1)
    middle = jnp.concatenate([xlo, x, xhi], axis=1)
    return jnp.concatenate([left, middle, right], axis=2)


def passed_along(x, axis, by):
    length = lax.axis_size(axis)
    pairs = [(i, i + by) for i in range(length) if 0 <= i + by < length]
    return lax.ppermute(x, axis, pairs)


def subzone_kernel(spots_ref, count_ref, block_a, mod_a, block_b, mod_b, total_ref,
                   um_ref, mur_ref, muis_ref, w1_ref, w2_ref, t_ref,
                   img1_ref, s1_ref, v3_ref, p_ref, q_ref):
    step = pl.program_id(0)
    lanes = block_a.shape[-1]
    half = lanes // 2
    group = half // 2
    first = 2 * step
    second = jnp.minimum(first + 1, count_ref[0] - 1)

    @pl.when(step == 0)
    def _():
        total_ref[...] = jnp.zeros_like(total_ref)
        w1_ref[...] = jnp.zeros_like(w1_ref)
        w2_ref[...] = jnp.zeros_like(w2_ref)
        t_ref[...] = jnp.zeros_like(t_ref)

    @pl.when(first < count_ref[0])
    def _():
        xa = spots_ref[first, 0]
        ya = pl.multiple_of(spots_ref[first, 1], HALO)
        za = spots_ref[first, 2]
        xb = spots_ref[second, 0]
        yb = pl.multiple_of(spots_ref[second, 1], HALO)
        zb = spots_ref[second, 2]
        lane = lax.broadcasted_iota(jnp.int32, (SUB, lanes), 1)
        depth = lane % half
        in_a = (lane % half) < group
        upper = lane >= half
        not_low = (lane % group) != 0
        not_high = (lane % group) != group - 1
        shift_a = (lanes - za) % lanes
        shift_b = (group - zb + lanes) % lanes

        def swap(v):
            return pltpu.roll(v, half, 1)

        def packed(ref_a, ref_b, k, x):
            a = ref_a[k, x].astype(jnp.float32)
            b = ref_b[k, x].astype(jnp.float32)
            return jnp.where(in_a, pltpu.roll(a, shift_a, 1), pltpu.roll(b, shift_b, 1))

        def laplace(ref, f, x):
            c = ref[f, x + 1, PADY:PADY + SUB, :]
            side = ref[f, x, PADY:PADY + SUB, :] + ref[f, x + 2, PADY:PADY + SUB, :]
            side = side + ref[f, x + 1, PADY - 1:PADY - 1 + SUB, :]
            side = side + ref[f, x + 1, PADY + 1:PADY + 1 + SUB, :]
            side = side + jnp.where(not_low, pltpu.roll(c, 1, 1), 0.0)
            side = side + jnp.where(not_high, pltpu.roll(c, lanes - 1, 1), 0.0)
            return 6.0 * c - side, c

        def stage_a(x, carry):
            mu = packed(mod_a, mod_b, 0, x)
            smu = swap(mu)
            mur_ref[x] = jnp.where(upper, smu, mu)
            muis_ref[x] = jnp.where(upper, mu, -smu)
            for f in range(NF):
                u = packed(block_a, block_b, f, x)
                um_ref[f, x] = u
                w1_ref[f, x + 1, PADY:PADY + SUB, :] = OMEGA * u
            return carry

        lax.fori_loop(0, SUB, stage_a, 0)

        def stage_b(x, carry):
            mur = mur_ref[x]
            muis = muis_ref[x]
            for f in range(NF):
                img, c = laplace(w1_ref, f, x)
                s = swap(img)
                u = um_ref[f, x]
                w2_ref[f, x + 1, PADY:PADY + SUB, :] = c + OMEGA * (u - c - (mur * img + muis * s))
                img1_ref[f, x] = img
                s1_ref[f, x] = s
            return carry

        lax.fori_loop(0, SUB, stage_b, 0)

        def stage_c(x, carry):
            mur = mur_ref[x]
            muis = muis_ref[x]
            pacc = jnp.zeros((SUB, lanes), jnp.float32)
            qacc = jnp.zeros((SUB, lanes), jnp.float32)
            for f in range(NF):
                img, c = laplace(w2_ref, f, x)
                s = swap(img)
                u = um_ref[f, x]
                w3 = c + OMEGA * (u - c - (mur * img + muis * s))
                v3 = w3 - u
                t_ref[f, x + 1, PADY:PADY + SUB, :] = mur * v3 - muis * swap(v3)
                v3_ref[f, x] = v3
                pacc = pacc + v3 * img
                qacc = qacc + v3 * s
            p_ref[x] = pacc
            q_ref[x] = qacc
            return carry

        lax.fori_loop(0, SUB, stage_c, 0)

        window_a = (depth >= za) & (depth < za + SUB)
        window_b = (depth >= zb) & (depth < zb + SUB)
        back_a = za % lanes
        back_b = (zb + lanes - group) % lanes
        live_b = first + 1 < count_ref[0]

        def stage_d(x, carry):
            pacc = p_ref[x]
            qacc = q_ref[x]
            for f in range(NF):
                lt, _ = laplace(t_ref, f, x)
                v3 = v3_ref[f, x]
                v2 = v3 - OMEGA * (v3 + lt)
                pacc = pacc + v2 * img1_ref[f, x]
                qacc = qacc + v2 * s1_ref[f, x]
            res = -OMEGA * jnp.where(upper, qacc - swap(qacc), pacc + swap(pacc))
            total_ref[xa + x, pl.ds(ya, SUB), :] += jnp.where(window_a, pltpu.roll(res, back_a, 1), 0.0)

            @pl.when(live_b)
            def _():
                total_ref[xb + x, pl.ds(yb, SUB), :] += jnp.where(window_b, pltpu.roll(res, back_b, 1), 0.0)

            return carry

        lax.fori_loop(0, SUB, stage_d, 0)


def subzone_pass(fields, modulus, spots, count, shift, extent):
    lanes = fields.shape[-1]
    home = spots.shape[0]
    ex, ey = extent

    def block_map(offset, base):
        def index(s, spots_ref, count_ref):
            live = jnp.minimum(2 * s + offset, jnp.maximum(count_ref[0] - 1, 0))
            row = jnp.clip(spots_ref[live, 0] - shift, 0, fields.shape[1] - SUB)
            col = jnp.clip(spots_ref[live, 1] - shift, 0, fields.shape[2] - SUB)
            col = pl.multiple_of(col, HALO)
            return (base, row, col, 0)
        return index

    f32 = jnp.float32
    padded = (NF, SUB + 2, SUB + 2 * PADY, lanes)
    block = (pl.Element(NF), pl.Element(SUB), pl.Element(SUB), pl.Element(lanes))
    mod_block = (pl.Element(1), pl.Element(SUB), pl.Element(SUB), pl.Element(lanes))
    base = modulus.shape[0] - 1
    grid_spec = pltpu.PrefetchScalarGridSpec(
        num_scalar_prefetch=2,
        grid=((home + 1) // 2,),
        in_specs=[
            pl.BlockSpec(block, block_map(0, 0)),
            pl.BlockSpec(mod_block, block_map(0, base)),
            pl.BlockSpec(block, block_map(1, 0)),
            pl.BlockSpec(mod_block, block_map(1, base)),
        ],
        out_specs=pl.BlockSpec((ex, ey, lanes), lambda s, spots_ref, count_ref: (0, 0, 0)),
        scratch_shapes=[
            pltpu.VMEM((NF, SUB, SUB, lanes), f32),
            pltpu.VMEM((SUB, SUB, lanes), f32),
            pltpu.VMEM((SUB, SUB, lanes), f32),
            pltpu.VMEM(padded, f32),
            pltpu.VMEM(padded, f32),
            pltpu.VMEM(padded, f32),
            pltpu.VMEM((NF, SUB, SUB, lanes), f32),
            pltpu.VMEM((NF, SUB, SUB, lanes), f32),
            pltpu.VMEM((NF, SUB, SUB, lanes), f32),
            pltpu.VMEM((SUB, SUB, lanes), f32),
            pltpu.VMEM((SUB, SUB, lanes), f32),
        ],
    )
    return pl.pallas_call(
        subzone_kernel,
        grid_spec=grid_spec,
        out_shape=jax.ShapeDtypeStruct((ex, ey, lanes), f32),
        cost_estimate=pl.CostEstimate(
            flops=STEP_FLOPS * ((home + 1) // 2), transcendentals=0, bytes_accessed=STEP_BYTES * ((home + 1) // 2)
        ),
        compiler_params=pltpu.CompilerParams(
            dimension_semantics=("arbitrary",), vmem_limit_bytes=100 * 1024 * 1024
        ),
    )(spots, count, fields, modulus, fields, modulus)


def shards(fields, modulus, anchors, home_count):
    home = anchors.shape[2]
    extent = (TX + 2 * HALO, TY + 2 * HALO)
    spots = (anchors[0, 0] * HALO).astype(jnp.int32)
    count = home_count[0, 0].astype(jnp.int32)
    slots = jnp.arange(home, dtype=jnp.int32)
    live = slots < count
    edge = ((spots[:, 0] < HALO) | (spots[:, 0] + SUB > TX + HALO)) & live
    side = (spots[:, 1] < HALO) | (spots[:, 1] + SUB > TY + HALO)
    inner = live & ~edge & ~side
    key = jnp.where(inner, 0, jnp.where(edge, 1, jnp.where(live, 2, 3)))
    order = jnp.argsort(key.astype(jnp.int32), stable=True)
    spots = spots[order]
    n_inner = jnp.sum(inner.astype(jnp.int32))
    n_edge = jnp.sum(edge.astype(jnp.int32))
    first = (n_inner // 2) * 2
    second = n_edge + n_inner % 2
    second = jnp.minimum(second + second % 2, count - first)
    middle_spots = jnp.take(spots, (slots + first) % home, axis=0)
    rest = jnp.take(spots, (slots + first + second) % home, axis=0)
    early = subzone_pass(fields, modulus[None], spots, first[None], HALO, extent)
    data = jnp.concatenate([fields, modulus[None]], axis=0)
    extended = with_halo(data, HALO)
    total = subzone_pass(extended, extended, middle_spots, second[None], 0, extent)
    late = subzone_pass(extended, extended, rest, (count - first - second)[None], 0, extent)
    from_above = passed_along(total[:HALO], "vx", -1)
    from_below = passed_along(total[TX + HALO :], "vx", 1)
    middle = total[HALO : HALO + TX] + late[HALO : HALO + TX] + early[HALO : HALO + TX]
    middle = middle.at[:HALO].add(from_below).at[TX - HALO :].add(from_above)
    from_right = passed_along(middle[:, :HALO], "vy", -1)
    from_left = passed_along(middle[:, TY + HALO :], "vy", 1)
    owned = middle[:, HALO : HALO + TY]
    owned = owned.at[:, :HALO].add(from_left).at[:, TY - HALO :].add(from_right)
    return owned


def solution(mesh):
    return jax.shard_map(
        shards,
        mesh=mesh,
        in_specs=(
            P(None, "vx", "vy", None),
            P("vx", "vy", None),
            P("vx", "vy", None, None),
            P("vx", "vy"),
        ),
        out_specs=P("vx", "vy", None),
        check_vma=False,
    )
```

```python
import functools

import jax
import jax.numpy as jnp
from jax import lax
from jax.experimental import pallas as pl
from jax.experimental.pallas import tpu as pltpu
from jax.sharding import PartitionSpec as P

NF = 4
SUB = 32
HALO = 16
TX = 64
TY = 160
RFWD = 3


OMEGA = 0.07
PADY = 8
STEP_FLOPS = 30_000_000_000
STEP_BYTES = 2 * (NF + 1) * SUB * SUB * 128 * 2


def with_halo(x, sides, width):
    for axis, dim in sides:
        size, length = (lax.axis_size(axis), x.shape[dim])
        up = [(i, (i + 1) % size) for i in range(size - 1)]
        down = [(j, i) for i, j in up]
        last = lax.slice_in_dim(x, length - width, length, axis=dim)
        first = lax.slice_in_dim(x, 0, width, axis=dim)
        before = lax.ppermute(last, axis, up)
        after = lax.ppermute(first, axis, down)
        x = jnp.concatenate([before, x, after], axis=dim)
    return x


def passed_along(x, axis, by):
    length = lax.axis_size(axis)
    pairs = [(i, i + by) for i in range(length) if 0 <= i + by < length]
    return lax.ppermute(x, axis, pairs)


def subzone_kernel(spots_ref, count_ref, block_a, mod_a, block_b, mod_b, total_ref,
                   um_ref, mur_ref, muis_ref, w1_ref, w2_ref, t_ref,
                   img1_ref, s1_ref, v3_ref, p_ref, q_ref):
    step = pl.program_id(0)
    lanes = block_a.shape[-1]
    half = lanes // 2
    group = half // 2
    first = 2 * step
    second = jnp.minimum(first + 1, count_ref[0] - 1)

    @pl.when(step == 0)
    def _():
        total_ref[...] = jnp.zeros_like(total_ref)
        w1_ref[...] = jnp.zeros_like(w1_ref)
        w2_ref[...] = jnp.zeros_like(w2_ref)
        t_ref[...] = jnp.zeros_like(t_ref)

    @pl.when(first < count_ref[0])
    def _():
        xa = spots_ref[first, 0]
        ya = pl.multiple_of(spots_ref[first, 1], HALO)
        za = spots_ref[first, 2]
        xb = spots_ref[second, 0]
        yb = pl.multiple_of(spots_ref[second, 1], HALO)
        zb = spots_ref[second, 2]
        lane = lax.broadcasted_iota(jnp.int32, (SUB, lanes), 1)
        depth = lane % half
        in_a = (lane % half) < group
        upper = lane >= half
        not_low = (lane % group) != 0
        not_high = (lane % group) != group - 1
        shift_a = (lanes - za) % lanes
        shift_b = (group - zb + lanes) % lanes

        def swap(v):
            return pltpu.roll(v, half, 1)

        def packed(ref_a, ref_b, k, x):
            a = ref_a[k, x].astype(jnp.float32)
            b = ref_b[k, x].astype(jnp.float32)
            return jnp.where(in_a, pltpu.roll(a, shift_a, 1), pltpu.roll(b, shift_b, 1))

        def laplace(ref, f, x):
            c = ref[f, x + 1, PADY:PADY + SUB, :]
            side = ref[f, x, PADY:PADY + SUB, :] + ref[f, x + 2, PADY:PADY + SUB, :]
            side = side + ref[f, x + 1, PADY - 1:PADY - 1 + SUB, :]
            side = side + ref[f, x + 1, PADY + 1:PADY + 1 + SUB, :]
            side = side + jnp.where(not_low, pltpu.roll(c, 1, 1), 0.0)
            side = side + jnp.where(not_high, pltpu.roll(c, lanes - 1, 1), 0.0)
            return 6.0 * c - side, c

        def stage_a(x, carry):
            mu = packed(mod_a, mod_b, 0, x)
            smu = swap(mu)
            mur_ref[x] = jnp.where(upper, smu, mu)
            muis_ref[x] = jnp.where(upper, mu, -smu)
            for f in range(NF):
                u = packed(block_a, block_b, f, x)
                um_ref[f, x] = u
                w1_ref[f, x + 1, PADY:PADY + SUB, :] = OMEGA * u
            return carry

        lax.fori_loop(0, SUB, stage_a, 0)

        def stage_b(x, carry):
            mur = mur_ref[x]
            muis = muis_ref[x]
            for f in range(NF):
                img, c = laplace(w1_ref, f, x)
                s = swap(img)
                u = um_ref[f, x]
                w2_ref[f, x + 1, PADY:PADY + SUB, :] = c + OMEGA * (u - c - (mur * img + muis * s))
                img1_ref[f, x] = img
                s1_ref[f, x] = s
            return carry

        lax.fori_loop(0, SUB, stage_b, 0)

        def stage_c(x, carry):
            mur = mur_ref[x]
            muis = muis_ref[x]
            pacc = jnp.zeros((SUB, lanes), jnp.float32)
            qacc = jnp.zeros((SUB, lanes), jnp.float32)
            for f in range(NF):
                img, c = laplace(w2_ref, f, x)
                s = swap(img)
                u = um_ref[f, x]
                w3 = c + OMEGA * (u - c - (mur * img + muis * s))
                v3 = w3 - u
                t_ref[f, x + 1, PADY:PADY + SUB, :] = mur * v3 - muis * swap(v3)
                v3_ref[f, x] = v3
                pacc = pacc + v3 * img
                qacc = qacc + v3 * s
            p_ref[x] = pacc
            q_ref[x] = qacc
            return carry

        lax.fori_loop(0, SUB, stage_c, 0)

        window_a = (depth >= za) & (depth < za + SUB)
        window_b = (depth >= zb) & (depth < zb + SUB)
        back_a = za % lanes
        back_b = (zb + lanes - group) % lanes
        live_b = first + 1 < count_ref[0]

        def stage_d(x, carry):
            pacc = p_ref[x]
            qacc = q_ref[x]
            for f in range(NF):
                lt, _ = laplace(t_ref, f, x)
                v3 = v3_ref[f, x]
                v2 = v3 - OMEGA * (v3 + lt)
                pacc = pacc + v2 * img1_ref[f, x]
                qacc = qacc + v2 * s1_ref[f, x]
            res = -OMEGA * jnp.where(upper, qacc - swap(qacc), pacc + swap(pacc))
            total_ref[xa + x, pl.ds(ya, SUB), :] += jnp.where(window_a, pltpu.roll(res, back_a, 1), 0.0)

            @pl.when(live_b)
            def _():
                total_ref[xb + x, pl.ds(yb, SUB), :] += jnp.where(window_b, pltpu.roll(res, back_b, 1), 0.0)

            return carry

        lax.fori_loop(0, SUB, stage_d, 0)


def subzone_pass(fields, modulus, spots, count, shift, extent):
    lanes = fields.shape[-1]
    home = spots.shape[0]
    ex, ey = extent

    def block_map(offset, base):
        def index(s, spots_ref, count_ref):
            live = jnp.minimum(2 * s + offset, jnp.maximum(count_ref[0] - 1, 0))
            row = jnp.clip(spots_ref[live, 0] - shift, 0, fields.shape[1] - SUB)
            col = jnp.clip(spots_ref[live, 1] - shift, 0, fields.shape[2] - SUB)
            col = pl.multiple_of(col, HALO)
            return (base, row, col, 0)
        return index

    f32 = jnp.float32
    padded = (NF, SUB + 2, SUB + 2 * PADY, lanes)
    block = (pl.Element(NF), pl.Element(SUB), pl.Element(SUB), pl.Element(lanes))
    mod_block = (pl.Element(1), pl.Element(SUB), pl.Element(SUB), pl.Element(lanes))
    base = modulus.shape[0] - 1
    grid_spec = pltpu.PrefetchScalarGridSpec(
        num_scalar_prefetch=2,
        grid=((home + 1) // 2,),
        in_specs=[
            pl.BlockSpec(block, block_map(0, 0)),
            pl.BlockSpec(mod_block, block_map(0, base)),
            pl.BlockSpec(block, block_map(1, 0)),
            pl.BlockSpec(mod_block, block_map(1, base)),
        ],
        out_specs=pl.BlockSpec((ex, ey, lanes), lambda s, spots_ref, count_ref: (0, 0, 0)),
        scratch_shapes=[
            pltpu.VMEM((NF, SUB, SUB, lanes), f32),
            pltpu.VMEM((SUB, SUB, lanes), f32),
            pltpu.VMEM((SUB, SUB, lanes), f32),
            pltpu.VMEM(padded, f32),
            pltpu.VMEM(padded, f32),
            pltpu.VMEM(padded, f32),
            pltpu.VMEM((NF, SUB, SUB, lanes), f32),
            pltpu.VMEM((NF, SUB, SUB, lanes), f32),
            pltpu.VMEM((NF, SUB, SUB, lanes), f32),
            pltpu.VMEM((SUB, SUB, lanes), f32),
            pltpu.VMEM((SUB, SUB, lanes), f32),
        ],
    )
    return pl.pallas_call(
        subzone_kernel,
        grid_spec=grid_spec,
        out_shape=jax.ShapeDtypeStruct((ex, ey, lanes), f32),
        cost_estimate=pl.CostEstimate(
            flops=STEP_FLOPS * ((home + 1) // 2), transcendentals=0, bytes_accessed=STEP_BYTES * ((home + 1) // 2)
        ),
        compiler_params=pltpu.CompilerParams(
            dimension_semantics=("arbitrary",), vmem_limit_bytes=100 * 1024 * 1024
        ),
    )(spots, count, fields, modulus, fields, modulus)


def shards(fields, modulus, anchors, home_count):
    home = anchors.shape[2]
    share = home // 2
    extent = (TX + 2 * HALO, TY + 2 * HALO)
    here = lax.axis_index("vx")
    last = lax.axis_size("vx") - 1
    spots = (anchors[0, 0] * HALO).astype(jnp.int32)
    count = home_count[0, 0].astype(jnp.int32)
    slots = jnp.arange(home, dtype=jnp.int32)
    live = slots < count
    low = live & (spots[:, 0] < HALO)
    high = live & (spots[:, 0] + SUB > TX + HALO)
    n_low = jnp.sum(low.astype(jnp.int32))
    n_high = jnp.sum(high.astype(jnp.int32))
    info = jnp.stack([count, n_low, n_high])
    prev = passed_along(info, "vx", 1)
    after = passed_along(info, "vx", -1)
    give_down = jnp.where(here > 0, jnp.minimum(n_low, jnp.clip((count - prev[0]) // 2, 0, share)), 0)
    give_up = jnp.where(here < last, jnp.minimum(n_high, jnp.clip((count - after[0]) // 2, 0, share)), 0)
    take_after = jnp.minimum(after[1], jnp.clip((after[0] - count) // 2, 0, share))
    take_prev = jnp.minimum(prev[2], jnp.clip((prev[0] - count) // 2, 0, share))
    low_spots = spots[jnp.argsort(jnp.where(low, 0, 1).astype(jnp.int32), stable=True)][:share]
    high_spots = spots[jnp.argsort(jnp.where(high, 0, 1).astype(jnp.int32), stable=True)][:share]
    from_after = passed_along(low_spots, "vx", -1) + jnp.array([TX, 0, 0], jnp.int32)
    from_prev = passed_along(high_spots, "vx", 1) - jnp.array([TX, 0, 0], jnp.int32)
    rank_low = jnp.cumsum(low.astype(jnp.int32)) - 1
    rank_high = jnp.cumsum(high.astype(jnp.int32)) - 1
    kept = live & ~(low & (rank_low < give_down)) & ~(high & (rank_high < give_up))
    edge = (low | high) & kept
    inner = kept & ~edge & (spots[:, 1] >= HALO) & (spots[:, 1] + SUB <= TY + HALO)
    near = jnp.arange(share, dtype=jnp.int32)
    all_spots = jnp.concatenate([spots, from_after, from_prev], axis=0)
    got = jnp.concatenate([near < take_after, near < take_prev])
    n_inner = jnp.sum(inner.astype(jnp.int32))
    first = (n_inner // 2) * 2
    rank = jnp.cumsum(inner.astype(jnp.int32)) - 1
    own_key = jnp.where(inner & (rank < first), 0, jnp.where(edge | (inner & (rank >= first)), 1,
                                                             jnp.where(kept, 2, 3)))
    key = jnp.concatenate([own_key, jnp.where(got, 1, 3)])
    order = jnp.argsort(key.astype(jnp.int32), stable=True)
    all_spots = all_spots[order]
    total_live = jnp.sum((key < 3).astype(jnp.int32))
    n_mid = jnp.sum((key == 1).astype(jnp.int32))
    second = jnp.minimum(n_mid + n_mid % 2, total_live - first)
    size = all_spots.shape[0]
    places = jnp.arange(size, dtype=jnp.int32)
    middle_spots = jnp.take(all_spots, (places + first) % size, axis=0)
    rest = jnp.take(all_spots, (places + first + second) % size, axis=0)
    early = subzone_pass(fields, modulus[None], all_spots, first[None], HALO, extent)
    data = jnp.concatenate([fields, modulus[None]], axis=0)
    extended = with_halo(data, (("vy", 2), ("vx", 1)), HALO)
    total = subzone_pass(extended, extended, middle_spots, second[None], 0, extent)
    late = subzone_pass(extended, extended, rest, (total_live - first - second)[None], 0, extent)
    from_above = passed_along(total[:HALO], "vx", -1)
    from_below = passed_along(total[TX + HALO :], "vx", 1)
    middle = total[HALO : HALO + TX] + late[HALO : HALO + TX] + early[HALO : HALO + TX]
    middle = middle.at[:HALO].add(from_below).at[TX - HALO :].add(from_above)
    from_right = passed_along(middle[:, :HALO], "vy", -1)
    from_left = passed_along(middle[:, TY + HALO :], "vy", 1)
    owned = middle[:, HALO : HALO + TY]
    owned = owned.at[:, :HALO].add(from_left).at[:, TY - HALO :].add(from_right)
    return owned


def solution(mesh):
    return jax.shard_map(
        shards,
        mesh=mesh,
        in_specs=(
            P(None, "vx", "vy", None),
            P("vx", "vy", None),
            P("vx", "vy", None, None),
            P("vx", "vy"),
        ),
        out_specs=P("vx", "vy", None),
        check_vma=False,
    )
```

```python
import functools

import jax
import jax.numpy as jnp
from jax import lax
from jax.experimental import pallas as pl
from jax.experimental.pallas import tpu as pltpu
from jax.sharding import PartitionSpec as P

NF = 4
SUB = 32
HALO = 16
TX = 64
TY = 160
RFWD = 3


OMEGA = 0.07
PADY = 8
STEP_FLOPS = 30_000_000_000
STEP_BYTES = 2 * (NF + 1) * SUB * SUB * 128 * 2


def with_halo(x, sides, width):
    for axis, dim in sides:
        size, length = (lax.axis_size(axis), x.shape[dim])
        up = [(i, (i + 1) % size) for i in range(size - 1)]
        down = [(j, i) for i, j in up]
        last = lax.slice_in_dim(x, length - width, length, axis=dim)
        first = lax.slice_in_dim(x, 0, width, axis=dim)
        before = lax.ppermute(last, axis, up)
        after = lax.ppermute(first, axis, down)
        x = jnp.concatenate([before, x, after], axis=dim)
    return x


def passed_along(x, axis, by):
    length = lax.axis_size(axis)
    pairs = [(i, i + by) for i in range(length) if 0 <= i + by < length]
    return lax.ppermute(x, axis, pairs)


def subzone_kernel(spots_ref, count_ref, block_a, mod_a, block_b, mod_b, total_ref,
                   um_ref, mur_ref, muis_ref, w1_ref, w2_ref, t_ref,
                   img1_ref, s1_ref, v3_ref, p_ref, q_ref):
    step = pl.program_id(0)
    lanes = block_a.shape[-1]
    half = lanes // 2
    group = half // 2
    first = 2 * step
    second = jnp.minimum(first + 1, count_ref[0] - 1)

    @pl.when(step == 0)
    def _():
        total_ref[...] = jnp.zeros_like(total_ref)
        w1_ref[...] = jnp.zeros_like(w1_ref)
        w2_ref[...] = jnp.zeros_like(w2_ref)
        t_ref[...] = jnp.zeros_like(t_ref)

    @pl.when(first < count_ref[0])
    def _():
        xa = spots_ref[first, 0]
        ya = pl.multiple_of(spots_ref[first, 1], HALO)
        za = spots_ref[first, 2]
        xb = spots_ref[second, 0]
        yb = pl.multiple_of(spots_ref[second, 1], HALO)
        zb = spots_ref[second, 2]
        lane = lax.broadcasted_iota(jnp.int32, (SUB, lanes), 1)
        depth = lane % half
        in_a = (lane % half) < group
        upper = lane >= half
        not_low = (lane % group) != 0
        not_high = (lane % group) != group - 1
        shift_a = (lanes - za) % lanes
        shift_b = (group - zb + lanes) % lanes

        def swap(v):
            return pltpu.roll(v, half, 1)

        def packed(ref_a, ref_b, k, x):
            a = ref_a[k, x].astype(jnp.float32)
            b = ref_b[k, x].astype(jnp.float32)
            return jnp.where(in_a, pltpu.roll(a, shift_a, 1), pltpu.roll(b, shift_b, 1))

        def laplace(ref, f, x):
            c = ref[f, x + 1, PADY:PADY + SUB, :]
            side = ref[f, x, PADY:PADY + SUB, :] + ref[f, x + 2, PADY:PADY + SUB, :]
            side = side + ref[f, x + 1, PADY - 1:PADY - 1 + SUB, :]
            side = side + ref[f, x + 1, PADY + 1:PADY + 1 + SUB, :]
            side = side + jnp.where(not_low, pltpu.roll(c, 1, 1), 0.0)
            side = side + jnp.where(not_high, pltpu.roll(c, lanes - 1, 1), 0.0)
            return 6.0 * c - side, c

        def stage_a(x, carry):
            mu = packed(mod_a, mod_b, 0, x)
            smu = swap(mu)
            mur_ref[x] = jnp.where(upper, smu, mu)
            muis_ref[x] = jnp.where(upper, mu, -smu)
            for f in range(NF):
                u = packed(block_a, block_b, f, x)
                um_ref[f, x] = u
                w1_ref[f, x + 1, PADY:PADY + SUB, :] = OMEGA * u
            return carry

        lax.fori_loop(0, SUB, stage_a, 0)

        def stage_b(x, carry):
            mur = mur_ref[x]
            muis = muis_ref[x]
            for f in range(NF):
                img, c = laplace(w1_ref, f, x)
                s = swap(img)
                u = um_ref[f, x]
                w2_ref[f, x + 1, PADY:PADY + SUB, :] = c + OMEGA * (u - c - (mur * img + muis * s))
                img1_ref[f, x] = img
                s1_ref[f, x] = s
            return carry

        lax.fori_loop(0, SUB, stage_b, 0)

        def stage_c(x, carry):
            mur = mur_ref[x]
            muis = muis_ref[x]
            pacc = jnp.zeros((SUB, lanes), jnp.float32)
            qacc = jnp.zeros((SUB, lanes), jnp.float32)
            for f in range(NF):
                img, c = laplace(w2_ref, f, x)
                s = swap(img)
                u = um_ref[f, x]
                w3 = c + OMEGA * (u - c - (mur * img + muis * s))
                v3 = w3 - u
                t_ref[f, x + 1, PADY:PADY + SUB, :] = mur * v3 - muis * swap(v3)
                v3_ref[f, x] = v3
                pacc = pacc + v3 * img
                qacc = qacc + v3 * s
            p_ref[x] = pacc
            q_ref[x] = qacc
            return carry

        lax.fori_loop(0, SUB, stage_c, 0)

        window_a = (depth >= za) & (depth < za + SUB)
        window_b = (depth >= zb) & (depth < zb + SUB)
        back_a = za % lanes
        back_b = (zb + lanes - group) % lanes
        live_b = first + 1 < count_ref[0]

        def stage_d(x, carry):
            pacc = p_ref[x]
            qacc = q_ref[x]
            for f in range(NF):
                lt, _ = laplace(t_ref, f, x)
                v3 = v3_ref[f, x]
                v2 = v3 - OMEGA * (v3 + lt)
                pacc = pacc + v2 * img1_ref[f, x]
                qacc = qacc + v2 * s1_ref[f, x]
            res = -OMEGA * jnp.where(upper, qacc - swap(qacc), pacc + swap(pacc))
            total_ref[xa + x, pl.ds(ya, SUB), :] += jnp.where(window_a, pltpu.roll(res, back_a, 1), 0.0)

            @pl.when(live_b)
            def _():
                total_ref[xb + x, pl.ds(yb, SUB), :] += jnp.where(window_b, pltpu.roll(res, back_b, 1), 0.0)

            return carry

        lax.fori_loop(0, SUB, stage_d, 0)


def subzone_pass(fields, modulus, spots, count, shift, extent):
    lanes = fields.shape[-1]
    home = spots.shape[0]
    ex, ey = extent

    def block_map(offset, base):
        def index(s, spots_ref, count_ref):
            live = jnp.minimum(2 * s + offset, jnp.maximum(count_ref[0] - 1, 0))
            row = jnp.clip(spots_ref[live, 0] - shift, 0, fields.shape[1] - SUB)
            col = jnp.clip(spots_ref[live, 1] - shift, 0, fields.shape[2] - SUB)
            col = pl.multiple_of(col, HALO)
            return (base, row, col, 0)
        return index

    f32 = jnp.float32
    padded = (NF, SUB + 2, SUB + 2 * PADY, lanes)
    block = (pl.Element(NF), pl.Element(SUB), pl.Element(SUB), pl.Element(lanes))
    mod_block = (pl.Element(1), pl.Element(SUB), pl.Element(SUB), pl.Element(lanes))
    base = modulus.shape[0] - 1
    grid_spec = pltpu.PrefetchScalarGridSpec(
        num_scalar_prefetch=2,
        grid=((home + 1) // 2,),
        in_specs=[
            pl.BlockSpec(block, block_map(0, 0)),
            pl.BlockSpec(mod_block, block_map(0, base)),
            pl.BlockSpec(block, block_map(1, 0)),
            pl.BlockSpec(mod_block, block_map(1, base)),
        ],
        out_specs=pl.BlockSpec((ex, ey, lanes), lambda s, spots_ref, count_ref: (0, 0, 0)),
        scratch_shapes=[
            pltpu.VMEM((NF, SUB, SUB, lanes), f32),
            pltpu.VMEM((SUB, SUB, lanes), f32),
            pltpu.VMEM((SUB, SUB, lanes), f32),
            pltpu.VMEM(padded, f32),
            pltpu.VMEM(padded, f32),
            pltpu.VMEM(padded, f32),
            pltpu.VMEM((NF, SUB, SUB, lanes), f32),
            pltpu.VMEM((NF, SUB, SUB, lanes), f32),
            pltpu.VMEM((NF, SUB, SUB, lanes), f32),
            pltpu.VMEM((SUB, SUB, lanes), f32),
            pltpu.VMEM((SUB, SUB, lanes), f32),
        ],
    )
    return pl.pallas_call(
        subzone_kernel,
        grid_spec=grid_spec,
        out_shape=jax.ShapeDtypeStruct((ex, ey, lanes), f32),
        cost_estimate=pl.CostEstimate(
            flops=STEP_FLOPS * ((home + 1) // 2), transcendentals=0, bytes_accessed=STEP_BYTES * ((home + 1) // 2)
        ),
        compiler_params=pltpu.CompilerParams(
            dimension_semantics=("arbitrary",), vmem_limit_bytes=100 * 1024 * 1024
        ),
    )(spots, count, fields, modulus, fields, modulus)


def shards(fields, modulus, anchors, home_count):
    home = anchors.shape[2]
    extent = (TX + 2 * HALO, TY + 2 * HALO)
    spots = (anchors[0, 0] * HALO).astype(jnp.int32)
    count = home_count[0, 0].astype(jnp.int32)
    slots = jnp.arange(home, dtype=jnp.int32)
    live = slots < count
    edge = ((spots[:, 0] < HALO) | (spots[:, 0] + SUB > TX + HALO)) & live
    side = (spots[:, 1] < HALO) | (spots[:, 1] + SUB > TY + HALO)
    inner = live & ~edge & ~side
    key = jnp.where(inner, 0, jnp.where(edge, 1, jnp.where(live, 2, 3)))
    order = jnp.argsort(key.astype(jnp.int32), stable=True)
    spots = spots[order]
    n_inner = jnp.sum(inner.astype(jnp.int32))
    n_edge = jnp.sum(edge.astype(jnp.int32))
    first = (n_inner // 2) * 2
    second = n_edge + n_inner % 2
    second = jnp.minimum(second + second % 2, count - first)
    middle_spots = jnp.take(spots, (slots + first) % home, axis=0)
    rest = jnp.take(spots, (slots + first + second) % home, axis=0)
    data = jnp.concatenate([fields, modulus[None]], axis=0)
    xlo = passed_along(data[:, TX - HALO :], "vx", 1)
    xhi = passed_along(data[:, :HALO], "vx", -1)
    ylo = passed_along(data[:, :, TY - HALO :], "vy", 1)
    yhi = passed_along(data[:, :, :HALO], "vy", -1)
    early = subzone_pass(fields, modulus[None], spots, first[None], HALO, extent)
    early, xlo, xhi = lax.optimization_barrier((early, xlo, xhi))
    to_right = jnp.concatenate([xlo[:, :, TY - HALO :], xhi[:, :, TY - HALO :]], axis=1)
    to_left = jnp.concatenate([xlo[:, :, :HALO], xhi[:, :, :HALO]], axis=1)
    from_left = passed_along(to_right, "vy", 1)
    from_right = passed_along(to_left, "vy", -1)
    wide = jnp.concatenate([ylo, data, yhi], axis=2)
    top = jnp.concatenate([from_left[:, :HALO], xlo, from_right[:, :HALO]], axis=2)
    bottom = jnp.concatenate([from_left[:, HALO:], xhi, from_right[:, HALO:]], axis=2)
    extended = jnp.concatenate([top, wide, bottom], axis=1)
    total = subzone_pass(extended, extended, middle_spots, second[None], 0, extent)
    late = subzone_pass(extended, extended, rest, (count - first - second)[None], 0, extent)
    from_above = passed_along(total[:HALO], "vx", -1)
    from_below = passed_along(total[TX + HALO :], "vx", 1)
    middle = total[HALO : HALO + TX] + late[HALO : HALO + TX] + early[HALO : HALO + TX]
    middle = middle.at[:HALO].add(from_below).at[TX - HALO :].add(from_above)
    from_right = passed_along(middle[:, :HALO], "vy", -1)
    from_left = passed_along(middle[:, TY + HALO :], "vy", 1)
    owned = middle[:, HALO : HALO + TY]
    owned = owned.at[:, :HALO].add(from_left).at[:, TY - HALO :].add(from_right)
    return owned


def solution(mesh):
    return jax.shard_map(
        shards,
        mesh=mesh,
        in_specs=(
            P(None, "vx", "vy", None),
            P("vx", "vy", None),
            P("vx", "vy", None, None),
            P("vx", "vy"),
        ),
        out_specs=P("vx", "vy", None),
        check_vma=False,
    )
```

```python
import functools

import jax
import jax.numpy as jnp
from jax import lax
from jax.experimental import pallas as pl
from jax.experimental.pallas import tpu as pltpu
from jax.sharding import PartitionSpec as P

NF = 4
SUB = 32
HALO = 16
TX = 64
TY = 160
RFWD = 3


OMEGA = 0.07
PADY = 8
STEP_FLOPS = 30_000_000_000
STEP_BYTES = 2 * (NF + 1) * SUB * SUB * 128 * 2


def with_halo(x, sides, width):
    for axis, dim in sides:
        size, length = (lax.axis_size(axis), x.shape[dim])
        up = [(i, (i + 1) % size) for i in range(size - 1)]
        down = [(j, i) for i, j in up]
        last = lax.slice_in_dim(x, length - width, length, axis=dim)
        first = lax.slice_in_dim(x, 0, width, axis=dim)
        before = lax.ppermute(last, axis, up)
        after = lax.ppermute(first, axis, down)
        x = jnp.concatenate([before, x, after], axis=dim)
    return x


def passed_along(x, axis, by):
    length = lax.axis_size(axis)
    pairs = [(i, i + by) for i in range(length) if 0 <= i + by < length]
    return lax.ppermute(x, axis, pairs)


def subzone_kernel(spots_ref, count_ref, block_a, mod_a, block_b, mod_b, total_ref,
                   um_ref, mur_ref, muis_ref, w1_ref, w2_ref, t_ref,
                   img1_ref, s1_ref, v3_ref, p_ref, q_ref):
    step = pl.program_id(0)
    lanes = block_a.shape[-1]
    half = lanes // 2
    group = half // 2
    first = 2 * step
    second = jnp.minimum(first + 1, count_ref[0] - 1)

    @pl.when(step == 0)
    def _():
        total_ref[...] = jnp.zeros_like(total_ref)
        w1_ref[...] = jnp.zeros_like(w1_ref)
        w2_ref[...] = jnp.zeros_like(w2_ref)
        t_ref[...] = jnp.zeros_like(t_ref)

    @pl.when(first < count_ref[0])
    def _():
        xa = spots_ref[first, 0]
        ya = pl.multiple_of(spots_ref[first, 1], HALO)
        za = spots_ref[first, 2]
        xb = spots_ref[second, 0]
        yb = pl.multiple_of(spots_ref[second, 1], HALO)
        zb = spots_ref[second, 2]
        lane = lax.broadcasted_iota(jnp.int32, (SUB, lanes), 1)
        depth = lane % half
        in_a = (lane % half) < group
        upper = lane >= half
        not_low = (lane % group) != 0
        not_high = (lane % group) != group - 1
        shift_a = (lanes - za) % lanes
        shift_b = (group - zb + lanes) % lanes

        def swap(v):
            return pltpu.roll(v, half, 1)

        def packed(ref_a, ref_b, k, x):
            a = ref_a[k, x].astype(jnp.float32)
            b = ref_b[k, x].astype(jnp.float32)
            return jnp.where(in_a, pltpu.roll(a, shift_a, 1), pltpu.roll(b, shift_b, 1))

        def laplace(ref, f, x):
            c = ref[f, x + 1, PADY:PADY + SUB, :]
            side = ref[f, x, PADY:PADY + SUB, :] + ref[f, x + 2, PADY:PADY + SUB, :]
            side = side + ref[f, x + 1, PADY - 1:PADY - 1 + SUB, :]
            side = side + ref[f, x + 1, PADY + 1:PADY + 1 + SUB, :]
            side = side + jnp.where(not_low, pltpu.roll(c, 1, 1), 0.0)
            side = side + jnp.where(not_high, pltpu.roll(c, lanes - 1, 1), 0.0)
            return 6.0 * c - side, c

        def stage_a(x, carry):
            mu = packed(mod_a, mod_b, 0, x)
            smu = swap(mu)
            mur_ref[x] = jnp.where(upper, smu, mu)
            muis_ref[x] = jnp.where(upper, mu, -smu)
            for f in range(NF):
                u = packed(block_a, block_b, f, x)
                um_ref[f, x] = u
                w1_ref[f, x + 1, PADY:PADY + SUB, :] = OMEGA * u
            return carry

        lax.fori_loop(0, SUB, stage_a, 0)

        def stage_b(x, carry):
            mur = mur_ref[x]
            muis = muis_ref[x]
            for f in range(NF):
                img, c = laplace(w1_ref, f, x)
                s = swap(img)
                u = um_ref[f, x]
                w2_ref[f, x + 1, PADY:PADY + SUB, :] = c + OMEGA * (u - c - (mur * img + muis * s))
                img1_ref[f, x] = img
                s1_ref[f, x] = s
            return carry

        lax.fori_loop(0, SUB, stage_b, 0)

        def stage_c(x, carry):
            mur = mur_ref[x]
            muis = muis_ref[x]
            pacc = jnp.zeros((SUB, lanes), jnp.float32)
            qacc = jnp.zeros((SUB, lanes), jnp.float32)
            for f in range(NF):
                img, c = laplace(w2_ref, f, x)
                s = swap(img)
                u = um_ref[f, x]
                w3 = c + OMEGA * (u - c - (mur * img + muis * s))
                v3 = w3 - u
                t_ref[f, x + 1, PADY:PADY + SUB, :] = mur * v3 - muis * swap(v3)
                v3_ref[f, x] = v3
                pacc = pacc + v3 * img
                qacc = qacc + v3 * s
            p_ref[x] = pacc
            q_ref[x] = qacc
            return carry

        lax.fori_loop(0, SUB, stage_c, 0)

        window_a = (depth >= za) & (depth < za + SUB)
        window_b = (depth >= zb) & (depth < zb + SUB)
        back_a = za % lanes
        back_b = (zb + lanes - group) % lanes
        live_b = first + 1 < count_ref[0]

        def stage_d(x, carry):
            pacc = p_ref[x]
            qacc = q_ref[x]
            for f in range(NF):
                lt, _ = laplace(t_ref, f, x)
                v3 = v3_ref[f, x]
                v2 = v3 - OMEGA * (v3 + lt)
                pacc = pacc + v2 * img1_ref[f, x]
                qacc = qacc + v2 * s1_ref[f, x]
            res = -OMEGA * jnp.where(upper, qacc - swap(qacc), pacc + swap(pacc))
            total_ref[xa + x, pl.ds(ya, SUB), :] += jnp.where(window_a, pltpu.roll(res, back_a, 1), 0.0)

            @pl.when(live_b)
            def _():
                total_ref[xb + x, pl.ds(yb, SUB), :] += jnp.where(window_b, pltpu.roll(res, back_b, 1), 0.0)

            return carry

        lax.fori_loop(0, SUB, stage_d, 0)


def subzone_pass(fields, modulus, spots, count, shift, extent):
    lanes = fields.shape[-1]
    home = spots.shape[0]
    ex, ey = extent

    def block_map(offset, base):
        def index(s, spots_ref, count_ref):
            live = jnp.minimum(2 * s + offset, jnp.maximum(count_ref[0] - 1, 0))
            row = jnp.clip(spots_ref[live, 0] - shift, 0, fields.shape[1] - SUB)
            col = jnp.clip(spots_ref[live, 1] - shift, 0, fields.shape[2] - SUB)
            col = pl.multiple_of(col, HALO)
            return (base, row, col, 0)
        return index

    f32 = jnp.float32
    padded = (NF, SUB + 2, SUB + 2 * PADY, lanes)
    block = (pl.Element(NF), pl.Element(SUB), pl.Element(SUB), pl.Element(lanes))
    mod_block = (pl.Element(1), pl.Element(SUB), pl.Element(SUB), pl.Element(lanes))
    base = modulus.shape[0] - 1
    grid_spec = pltpu.PrefetchScalarGridSpec(
        num_scalar_prefetch=2,
        grid=((home + 1) // 2,),
        in_specs=[
            pl.BlockSpec(block, block_map(0, 0)),
            pl.BlockSpec(mod_block, block_map(0, base)),
            pl.BlockSpec(block, block_map(1, 0)),
            pl.BlockSpec(mod_block, block_map(1, base)),
        ],
        out_specs=pl.BlockSpec((ex, ey, lanes), lambda s, spots_ref, count_ref: (0, 0, 0)),
        scratch_shapes=[
            pltpu.VMEM((NF, SUB, SUB, lanes), f32),
            pltpu.VMEM((SUB, SUB, lanes), f32),
            pltpu.VMEM((SUB, SUB, lanes), f32),
            pltpu.VMEM(padded, f32),
            pltpu.VMEM(padded, f32),
            pltpu.VMEM(padded, f32),
            pltpu.VMEM((NF, SUB, SUB, lanes), f32),
            pltpu.VMEM((NF, SUB, SUB, lanes), f32),
            pltpu.VMEM((NF, SUB, SUB, lanes), f32),
            pltpu.VMEM((SUB, SUB, lanes), f32),
            pltpu.VMEM((SUB, SUB, lanes), f32),
        ],
    )
    return pl.pallas_call(
        subzone_kernel,
        grid_spec=grid_spec,
        out_shape=jax.ShapeDtypeStruct((ex, ey, lanes), f32),
        cost_estimate=pl.CostEstimate(
            flops=STEP_FLOPS * ((home + 1) // 2), transcendentals=0, bytes_accessed=STEP_BYTES * ((home + 1) // 2)
        ),
        compiler_params=pltpu.CompilerParams(
            dimension_semantics=("arbitrary",), vmem_limit_bytes=100 * 1024 * 1024
        ),
    )(spots, count, fields, modulus, fields, modulus)


def shards(fields, modulus, anchors, home_count):
    home = anchors.shape[2]
    extent = (TX + 2 * HALO, TY + 2 * HALO)
    spots = (anchors[0, 0] * HALO).astype(jnp.int32)
    count = home_count[0, 0].astype(jnp.int32)
    slots = jnp.arange(home, dtype=jnp.int32)
    live = slots < count
    edge = ((spots[:, 0] < HALO) | (spots[:, 0] + SUB > TX + HALO)) & live
    side = (spots[:, 1] < HALO) | (spots[:, 1] + SUB > TY + HALO)
    inner = live & ~edge & ~side
    key = jnp.where(inner, 0, jnp.where(edge, 1, jnp.where(live, 2, 3)))
    order = jnp.argsort(key.astype(jnp.int32), stable=True)
    spots = spots[order]
    n_inner = jnp.sum(inner.astype(jnp.int32))
    n_edge = jnp.sum(edge.astype(jnp.int32))
    first = (n_inner // 2) * 2
    second = n_edge + n_inner % 2
    second = jnp.minimum(second + second % 2, count - first)
    middle_spots = jnp.take(spots, (slots + first) % home, axis=0)
    rest = jnp.take(spots, (slots + first + second) % home, axis=0)
    data = jnp.concatenate([fields, modulus[None]], axis=0)
    xlo = passed_along(data[:, TX - HALO :], "vx", 1)
    xhi = passed_along(data[:, :HALO], "vx", -1)
    ylo = passed_along(data[:, :, TY - HALO :], "vy", 1)
    yhi = passed_along(data[:, :, :HALO], "vy", -1)
    early = subzone_pass(fields, modulus[None], spots, first[None], HALO, extent)
    early, xlo, xhi = lax.optimization_barrier((early, xlo, xhi))
    to_right = jnp.concatenate([xlo[:, :, TY - HALO :], xhi[:, :, TY - HALO :]], axis=1)
    to_left = jnp.concatenate([xlo[:, :, :HALO], xhi[:, :, :HALO]], axis=1)
    from_left = passed_along(to_right, "vy", 1)
    from_right = passed_along(to_left, "vy", -1)
    wide = lax.optimization_barrier(jnp.concatenate([ylo, data, yhi], axis=2))
    top = jnp.concatenate([from_left[:, :HALO], xlo, from_right[:, :HALO]], axis=2)
    bottom = jnp.concatenate([from_left[:, HALO:], xhi, from_right[:, HALO:]], axis=2)
    top, bottom = lax.optimization_barrier((top, bottom))
    extended = jnp.concatenate([top, wide, bottom], axis=1)
    total = subzone_pass(extended, extended, middle_spots, second[None], 0, extent)
    late = subzone_pass(extended, extended, rest, (count - first - second)[None], 0, extent)
    from_above = passed_along(total[:HALO], "vx", -1)
    from_below = passed_along(total[TX + HALO :], "vx", 1)
    middle = total[HALO : HALO + TX] + late[HALO : HALO + TX] + early[HALO : HALO + TX]
    middle = middle.at[:HALO].add(from_below).at[TX - HALO :].add(from_above)
    from_right = passed_along(middle[:, :HALO], "vy", -1)
    from_left = passed_along(middle[:, TY + HALO :], "vy", 1)
    owned = middle[:, HALO : HALO + TY]
    owned = owned.at[:, :HALO].add(from_left).at[:, TY - HALO :].add(from_right)
    return owned


def solution(mesh):
    return jax.shard_map(
        shards,
        mesh=mesh,
        in_specs=(
            P(None, "vx", "vy", None),
            P("vx", "vy", None),
            P("vx", "vy", None, None),
            P("vx", "vy"),
        ),
        out_specs=P("vx", "vy", None),
        check_vma=False,
    )
```

```python
import functools

import jax
import jax.numpy as jnp
from jax import lax
from jax.experimental import pallas as pl
from jax.experimental.pallas import tpu as pltpu
from jax.sharding import PartitionSpec as P

NF = 4
SUB = 32
HALO = 16
TX = 64
TY = 160
RFWD = 3


OMEGA = 0.07
PADY = 8
EARLY = 6
STEP_FLOPS = 30_000_000_000
STEP_BYTES = 2 * (NF + 1) * SUB * SUB * 128 * 2


def with_halo(x, sides, width):
    for axis, dim in sides:
        size, length = (lax.axis_size(axis), x.shape[dim])
        up = [(i, (i + 1) % size) for i in range(size - 1)]
        down = [(j, i) for i, j in up]
        last = lax.slice_in_dim(x, length - width, length, axis=dim)
        first = lax.slice_in_dim(x, 0, width, axis=dim)
        before = lax.ppermute(last, axis, up)
        after = lax.ppermute(first, axis, down)
        x = jnp.concatenate([before, x, after], axis=dim)
    return x


def passed_along(x, axis, by):
    length = lax.axis_size(axis)
    pairs = [(i, i + by) for i in range(length) if 0 <= i + by < length]
    return lax.ppermute(x, axis, pairs)


def subzone_kernel(spots_ref, count_ref, block_a, mod_a, block_b, mod_b, total_ref,
                   um_ref, mur_ref, muis_ref, w1_ref, w2_ref, t_ref,
                   img1_ref, s1_ref, v3_ref, p_ref, q_ref):
    step = pl.program_id(0)
    lanes = block_a.shape[-1]
    half = lanes // 2
    group = half // 2
    first = 2 * step
    second = jnp.minimum(first + 1, count_ref[0] - 1)

    @pl.when(step == 0)
    def _():
        total_ref[...] = jnp.zeros_like(total_ref)
        w1_ref[...] = jnp.zeros_like(w1_ref)
        w2_ref[...] = jnp.zeros_like(w2_ref)
        t_ref[...] = jnp.zeros_like(t_ref)

    @pl.when(first < count_ref[0])
    def _():
        xa = spots_ref[first, 0]
        ya = pl.multiple_of(spots_ref[first, 1], HALO)
        za = spots_ref[first, 2]
        xb = spots_ref[second, 0]
        yb = pl.multiple_of(spots_ref[second, 1], HALO)
        zb = spots_ref[second, 2]
        lane = lax.broadcasted_iota(jnp.int32, (SUB, lanes), 1)
        depth = lane % half
        in_a = (lane % half) < group
        upper = lane >= half
        not_low = (lane % group) != 0
        not_high = (lane % group) != group - 1
        shift_a = (lanes - za) % lanes
        shift_b = (group - zb + lanes) % lanes

        def swap(v):
            return pltpu.roll(v, half, 1)

        def packed(ref_a, ref_b, k, x):
            a = ref_a[k, x].astype(jnp.float32)
            b = ref_b[k, x].astype(jnp.float32)
            return jnp.where(in_a, pltpu.roll(a, shift_a, 1), pltpu.roll(b, shift_b, 1))

        def laplace(ref, f, x):
            c = ref[f, x + 1, PADY:PADY + SUB, :]
            side = ref[f, x, PADY:PADY + SUB, :] + ref[f, x + 2, PADY:PADY + SUB, :]
            side = side + ref[f, x + 1, PADY - 1:PADY - 1 + SUB, :]
            side = side + ref[f, x + 1, PADY + 1:PADY + 1 + SUB, :]
            side = side + jnp.where(not_low, pltpu.roll(c, 1, 1), 0.0)
            side = side + jnp.where(not_high, pltpu.roll(c, lanes - 1, 1), 0.0)
            return 6.0 * c - side, c

        def stage_a(x, carry):
            mu = packed(mod_a, mod_b, 0, x)
            smu = swap(mu)
            mur_ref[x] = jnp.where(upper, smu, mu)
            muis_ref[x] = jnp.where(upper, mu, -smu)
            for f in range(NF):
                u = packed(block_a, block_b, f, x)
                um_ref[f, x] = u
                w1_ref[f, x + 1, PADY:PADY + SUB, :] = OMEGA * u
            return carry

        lax.fori_loop(0, SUB, stage_a, 0)

        def stage_b(x, carry):
            mur = mur_ref[x]
            muis = muis_ref[x]
            for f in range(NF):
                img, c = laplace(w1_ref, f, x)
                s = swap(img)
                u = um_ref[f, x]
                w2_ref[f, x + 1, PADY:PADY + SUB, :] = c + OMEGA * (u - c - (mur * img + muis * s))
                img1_ref[f, x] = img
                s1_ref[f, x] = s
            return carry

        lax.fori_loop(0, SUB, stage_b, 0)

        def stage_c(x, carry):
            mur = mur_ref[x]
            muis = muis_ref[x]
            pacc = jnp.zeros((SUB, lanes), jnp.float32)
            qacc = jnp.zeros((SUB, lanes), jnp.float32)
            for f in range(NF):
                img, c = laplace(w2_ref, f, x)
                s = swap(img)
                u = um_ref[f, x]
                w3 = c + OMEGA * (u - c - (mur * img + muis * s))
                v3 = w3 - u
                t_ref[f, x + 1, PADY:PADY + SUB, :] = mur * v3 - muis * swap(v3)
                v3_ref[f, x] = v3
                pacc = pacc + v3 * img
                qacc = qacc + v3 * s
            p_ref[x] = pacc
            q_ref[x] = qacc
            return carry

        lax.fori_loop(0, SUB, stage_c, 0)

        window_a = (depth >= za) & (depth < za + SUB)
        window_b = (depth >= zb) & (depth < zb + SUB)
        back_a = za % lanes
        back_b = (zb + lanes - group) % lanes
        live_b = first + 1 < count_ref[0]

        def stage_d(x, carry):
            pacc = p_ref[x]
            qacc = q_ref[x]
            for f in range(NF):
                lt, _ = laplace(t_ref, f, x)
                v3 = v3_ref[f, x]
                v2 = v3 - OMEGA * (v3 + lt)
                pacc = pacc + v2 * img1_ref[f, x]
                qacc = qacc + v2 * s1_ref[f, x]
            res = -OMEGA * jnp.where(upper, qacc - swap(qacc), pacc + swap(pacc))
            total_ref[xa + x, pl.ds(ya, SUB), :] += jnp.where(window_a, pltpu.roll(res, back_a, 1), 0.0)

            @pl.when(live_b)
            def _():
                total_ref[xb + x, pl.ds(yb, SUB), :] += jnp.where(window_b, pltpu.roll(res, back_b, 1), 0.0)

            return carry

        lax.fori_loop(0, SUB, stage_d, 0)


def subzone_pass(fields, modulus, spots, count, shift, extent):
    lanes = fields.shape[-1]
    home = spots.shape[0]
    ex, ey = extent

    def block_map(offset, base):
        def index(s, spots_ref, count_ref):
            live = jnp.minimum(2 * s + offset, jnp.maximum(count_ref[0] - 1, 0))
            row = jnp.clip(spots_ref[live, 0] - shift, 0, fields.shape[1] - SUB)
            col = jnp.clip(spots_ref[live, 1] - shift, 0, fields.shape[2] - SUB)
            col = pl.multiple_of(col, HALO)
            return (base, row, col, 0)
        return index

    f32 = jnp.float32
    padded = (NF, SUB + 2, SUB + 2 * PADY, lanes)
    block = (pl.Element(NF), pl.Element(SUB), pl.Element(SUB), pl.Element(lanes))
    mod_block = (pl.Element(1), pl.Element(SUB), pl.Element(SUB), pl.Element(lanes))
    base = modulus.shape[0] - 1
    grid_spec = pltpu.PrefetchScalarGridSpec(
        num_scalar_prefetch=2,
        grid=((home + 1) // 2,),
        in_specs=[
            pl.BlockSpec(block, block_map(0, 0)),
            pl.BlockSpec(mod_block, block_map(0, base)),
            pl.BlockSpec(block, block_map(1, 0)),
            pl.BlockSpec(mod_block, block_map(1, base)),
        ],
        out_specs=pl.BlockSpec((ex, ey, lanes), lambda s, spots_ref, count_ref: (0, 0, 0)),
        scratch_shapes=[
            pltpu.VMEM((NF, SUB, SUB, lanes), f32),
            pltpu.VMEM((SUB, SUB, lanes), f32),
            pltpu.VMEM((SUB, SUB, lanes), f32),
            pltpu.VMEM(padded, f32),
            pltpu.VMEM(padded, f32),
            pltpu.VMEM(padded, f32),
            pltpu.VMEM((NF, SUB, SUB, lanes), f32),
            pltpu.VMEM((NF, SUB, SUB, lanes), f32),
            pltpu.VMEM((NF, SUB, SUB, lanes), f32),
            pltpu.VMEM((SUB, SUB, lanes), f32),
            pltpu.VMEM((SUB, SUB, lanes), f32),
        ],
    )
    return pl.pallas_call(
        subzone_kernel,
        grid_spec=grid_spec,
        out_shape=jax.ShapeDtypeStruct((ex, ey, lanes), f32),
        cost_estimate=pl.CostEstimate(
            flops=STEP_FLOPS * ((home + 1) // 2), transcendentals=0, bytes_accessed=STEP_BYTES * ((home + 1) // 2)
        ),
        compiler_params=pltpu.CompilerParams(
            dimension_semantics=("arbitrary",), vmem_limit_bytes=100 * 1024 * 1024
        ),
    )(spots, count, fields, modulus, fields, modulus)


def shards(fields, modulus, anchors, home_count):
    home = anchors.shape[2]
    extent = (TX + 2 * HALO, TY + 2 * HALO)
    spots = (anchors[0, 0] * HALO).astype(jnp.int32)
    count = home_count[0, 0].astype(jnp.int32)
    slots = jnp.arange(home, dtype=jnp.int32)
    live = slots < count
    edge = ((spots[:, 0] < HALO) | (spots[:, 0] + SUB > TX + HALO)) & live
    side = (spots[:, 1] < HALO) | (spots[:, 1] + SUB > TY + HALO)
    inner = live & ~edge & ~side
    n_inner = jnp.sum(inner.astype(jnp.int32))
    n_edge = jnp.sum(edge.astype(jnp.int32))
    first = jnp.minimum(EARLY, (n_inner // 2) * 2)
    rank = jnp.cumsum(inner.astype(jnp.int32)) - 1
    key = jnp.where(inner & (rank < first), 0, jnp.where(edge, 1, jnp.where(live, 2, 3)))
    order = jnp.argsort(key.astype(jnp.int32), stable=True)
    spots = spots[order]
    second = jnp.minimum(n_edge + n_edge % 2, count - first)
    middle_spots = jnp.take(spots, (slots + first) % home, axis=0)
    rest = jnp.take(spots, (slots + first + second) % home, axis=0)
    early = subzone_pass(fields, modulus[None], spots, first[None], HALO, extent)
    data = jnp.concatenate([fields, modulus[None]], axis=0)
    extended = with_halo(data, (("vy", 2), ("vx", 1)), HALO)
    total = subzone_pass(extended, extended, middle_spots, second[None], 0, extent)
    late = subzone_pass(extended, extended, rest, (count - first - second)[None], 0, extent)
    from_above = passed_along(total[:HALO], "vx", -1)
    from_below = passed_along(total[TX + HALO :], "vx", 1)
    middle = total[HALO : HALO + TX] + late[HALO : HALO + TX] + early[HALO : HALO + TX]
    middle = middle.at[:HALO].add(from_below).at[TX - HALO :].add(from_above)
    from_right = passed_along(middle[:, :HALO], "vy", -1)
    from_left = passed_along(middle[:, TY + HALO :], "vy", 1)
    owned = middle[:, HALO : HALO + TY]
    owned = owned.at[:, :HALO].add(from_left).at[:, TY - HALO :].add(from_right)
    return owned


def solution(mesh):
    return jax.shard_map(
        shards,
        mesh=mesh,
        in_specs=(
            P(None, "vx", "vy", None),
            P("vx", "vy", None),
            P("vx", "vy", None, None),
            P("vx", "vy"),
        ),
        out_specs=P("vx", "vy", None),
        check_vma=False,
    )
```

```python
import functools

import jax
import jax.numpy as jnp
from jax import lax
from jax.experimental import pallas as pl
from jax.experimental.pallas import tpu as pltpu
from jax.sharding import PartitionSpec as P

NF = 4
SUB = 32
HALO = 16
TX = 64
TY = 160
RFWD = 3


OMEGA = 0.07
PADY = 8
LATE = 2
STEP_FLOPS = 30_000_000_000
STEP_BYTES = 2 * (NF + 1) * SUB * SUB * 128 * 2


def with_halo(x, sides, width):
    for axis, dim in sides:
        size, length = (lax.axis_size(axis), x.shape[dim])
        up = [(i, (i + 1) % size) for i in range(size - 1)]
        down = [(j, i) for i, j in up]
        last = lax.slice_in_dim(x, length - width, length, axis=dim)
        first = lax.slice_in_dim(x, 0, width, axis=dim)
        before = lax.ppermute(last, axis, up)
        after = lax.ppermute(first, axis, down)
        x = jnp.concatenate([before, x, after], axis=dim)
    return x


def passed_along(x, axis, by):
    length = lax.axis_size(axis)
    pairs = [(i, i + by) for i in range(length) if 0 <= i + by < length]
    return lax.ppermute(x, axis, pairs)


def subzone_kernel(spots_ref, count_ref, block_a, mod_a, block_b, mod_b, total_ref,
                   um_ref, mur_ref, muis_ref, w1_ref, w2_ref, t_ref,
                   img1_ref, s1_ref, v3_ref, p_ref, q_ref):
    step = pl.program_id(0)
    lanes = block_a.shape[-1]
    half = lanes // 2
    group = half // 2
    first = 2 * step
    second = jnp.minimum(first + 1, count_ref[0] - 1)

    @pl.when(step == 0)
    def _():
        total_ref[...] = jnp.zeros_like(total_ref)
        w1_ref[...] = jnp.zeros_like(w1_ref)
        w2_ref[...] = jnp.zeros_like(w2_ref)
        t_ref[...] = jnp.zeros_like(t_ref)

    @pl.when(first < count_ref[0])
    def _():
        xa = spots_ref[first, 0]
        ya = pl.multiple_of(spots_ref[first, 1], HALO)
        za = spots_ref[first, 2]
        xb = spots_ref[second, 0]
        yb = pl.multiple_of(spots_ref[second, 1], HALO)
        zb = spots_ref[second, 2]
        lane = lax.broadcasted_iota(jnp.int32, (SUB, lanes), 1)
        depth = lane % half
        in_a = (lane % half) < group
        upper = lane >= half
        not_low = (lane % group) != 0
        not_high = (lane % group) != group - 1
        shift_a = (lanes - za) % lanes
        shift_b = (group - zb + lanes) % lanes

        def swap(v):
            return pltpu.roll(v, half, 1)

        def packed(ref_a, ref_b, k, x):
            a = ref_a[k, x].astype(jnp.float32)
            b = ref_b[k, x].astype(jnp.float32)
            return jnp.where(in_a, pltpu.roll(a, shift_a, 1), pltpu.roll(b, shift_b, 1))

        def laplace(ref, f, x):
            c = ref[f, x + 1, PADY:PADY + SUB, :]
            side = ref[f, x, PADY:PADY + SUB, :] + ref[f, x + 2, PADY:PADY + SUB, :]
            side = side + ref[f, x + 1, PADY - 1:PADY - 1 + SUB, :]
            side = side + ref[f, x + 1, PADY + 1:PADY + 1 + SUB, :]
            side = side + jnp.where(not_low, pltpu.roll(c, 1, 1), 0.0)
            side = side + jnp.where(not_high, pltpu.roll(c, lanes - 1, 1), 0.0)
            return 6.0 * c - side, c

        def stage_a(x, carry):
            mu = packed(mod_a, mod_b, 0, x)
            smu = swap(mu)
            mur_ref[x] = jnp.where(upper, smu, mu)
            muis_ref[x] = jnp.where(upper, mu, -smu)
            for f in range(NF):
                u = packed(block_a, block_b, f, x)
                um_ref[f, x] = u
                w1_ref[f, x + 1, PADY:PADY + SUB, :] = OMEGA * u
            return carry

        lax.fori_loop(0, SUB, stage_a, 0)

        def stage_b(x, carry):
            mur = mur_ref[x]
            muis = muis_ref[x]
            for f in range(NF):
                img, c = laplace(w1_ref, f, x)
                s = swap(img)
                u = um_ref[f, x]
                w2_ref[f, x + 1, PADY:PADY + SUB, :] = c + OMEGA * (u - c - (mur * img + muis * s))
                img1_ref[f, x] = img
                s1_ref[f, x] = s
            return carry

        lax.fori_loop(0, SUB, stage_b, 0)

        def stage_c(x, carry):
            mur = mur_ref[x]
            muis = muis_ref[x]
            pacc = jnp.zeros((SUB, lanes), jnp.float32)
            qacc = jnp.zeros((SUB, lanes), jnp.float32)
            for f in range(NF):
                img, c = laplace(w2_ref, f, x)
                s = swap(img)
                u = um_ref[f, x]
                w3 = c + OMEGA * (u - c - (mur * img + muis * s))
                v3 = w3 - u
                t_ref[f, x + 1, PADY:PADY + SUB, :] = mur * v3 - muis * swap(v3)
                v3_ref[f, x] = v3
                pacc = pacc + v3 * img
                qacc = qacc + v3 * s
            p_ref[x] = pacc
            q_ref[x] = qacc
            return carry

        lax.fori_loop(0, SUB, stage_c, 0)

        window_a = (depth >= za) & (depth < za + SUB)
        window_b = (depth >= zb) & (depth < zb + SUB)
        back_a = za % lanes
        back_b = (zb + lanes - group) % lanes
        live_b = first + 1 < count_ref[0]

        def stage_d(x, carry):
            pacc = p_ref[x]
            qacc = q_ref[x]
            for f in range(NF):
                lt, _ = laplace(t_ref, f, x)
                v3 = v3_ref[f, x]
                v2 = v3 - OMEGA * (v3 + lt)
                pacc = pacc + v2 * img1_ref[f, x]
                qacc = qacc + v2 * s1_ref[f, x]
            res = -OMEGA * jnp.where(upper, qacc - swap(qacc), pacc + swap(pacc))
            total_ref[xa + x, pl.ds(ya, SUB), :] += jnp.where(window_a, pltpu.roll(res, back_a, 1), 0.0)

            @pl.when(live_b)
            def _():
                total_ref[xb + x, pl.ds(yb, SUB), :] += jnp.where(window_b, pltpu.roll(res, back_b, 1), 0.0)

            return carry

        lax.fori_loop(0, SUB, stage_d, 0)


def subzone_pass(fields, modulus, spots, count, shift, extent):
    lanes = fields.shape[-1]
    home = spots.shape[0]
    ex, ey = extent

    def block_map(offset, base):
        def index(s, spots_ref, count_ref):
            live = jnp.minimum(2 * s + offset, jnp.maximum(count_ref[0] - 1, 0))
            row = jnp.clip(spots_ref[live, 0] - shift, 0, fields.shape[1] - SUB)
            col = jnp.clip(spots_ref[live, 1] - shift, 0, fields.shape[2] - SUB)
            col = pl.multiple_of(col, HALO)
            return (base, row, col, 0)
        return index

    f32 = jnp.float32
    padded = (NF, SUB + 2, SUB + 2 * PADY, lanes)
    block = (pl.Element(NF), pl.Element(SUB), pl.Element(SUB), pl.Element(lanes))
    mod_block = (pl.Element(1), pl.Element(SUB), pl.Element(SUB), pl.Element(lanes))
    base = modulus.shape[0] - 1
    grid_spec = pltpu.PrefetchScalarGridSpec(
        num_scalar_prefetch=2,
        grid=((home + 1) // 2,),
        in_specs=[
            pl.BlockSpec(block, block_map(0, 0)),
            pl.BlockSpec(mod_block, block_map(0, base)),
            pl.BlockSpec(block, block_map(1, 0)),
            pl.BlockSpec(mod_block, block_map(1, base)),
        ],
        out_specs=pl.BlockSpec((ex, ey, lanes), lambda s, spots_ref, count_ref: (0, 0, 0)),
        scratch_shapes=[
            pltpu.VMEM((NF, SUB, SUB, lanes), f32),
            pltpu.VMEM((SUB, SUB, lanes), f32),
            pltpu.VMEM((SUB, SUB, lanes), f32),
            pltpu.VMEM(padded, f32),
            pltpu.VMEM(padded, f32),
            pltpu.VMEM(padded, f32),
            pltpu.VMEM((NF, SUB, SUB, lanes), f32),
            pltpu.VMEM((NF, SUB, SUB, lanes), f32),
            pltpu.VMEM((NF, SUB, SUB, lanes), f32),
            pltpu.VMEM((SUB, SUB, lanes), f32),
            pltpu.VMEM((SUB, SUB, lanes), f32),
        ],
    )
    return pl.pallas_call(
        subzone_kernel,
        grid_spec=grid_spec,
        out_shape=jax.ShapeDtypeStruct((ex, ey, lanes), f32),
        cost_estimate=pl.CostEstimate(
            flops=STEP_FLOPS * ((home + 1) // 2), transcendentals=0, bytes_accessed=STEP_BYTES * ((home + 1) // 2)
        ),
        compiler_params=pltpu.CompilerParams(
            dimension_semantics=("arbitrary",), vmem_limit_bytes=100 * 1024 * 1024
        ),
    )(spots, count, fields, modulus, fields, modulus)


def shards(fields, modulus, anchors, home_count):
    home = anchors.shape[2]
    extent = (TX + 2 * HALO, TY + 2 * HALO)
    spots = (anchors[0, 0] * HALO).astype(jnp.int32)
    count = home_count[0, 0].astype(jnp.int32)
    slots = jnp.arange(home, dtype=jnp.int32)
    live = slots < count
    edge = ((spots[:, 0] < HALO) | (spots[:, 0] + SUB > TX + HALO)) & live
    side = (spots[:, 1] < HALO) | (spots[:, 1] + SUB > TY + HALO)
    inner = live & ~edge & ~side
    key = jnp.where(inner, 0, jnp.where(edge, 1, jnp.where(live, 2, 3)))
    order = jnp.argsort(key.astype(jnp.int32), stable=True)
    spots = spots[order]
    n_inner = jnp.sum(inner.astype(jnp.int32))
    n_edge = jnp.sum(edge.astype(jnp.int32))
    first = (n_inner // 2) * 2
    late_n = jnp.clip(count - first - n_edge - n_inner % 2, 0, LATE)
    late_n = late_n - jnp.where((late_n > 0) & ((count - first - late_n) % 2 == 1), 1, 0)
    second = count - first - late_n
    middle_spots = jnp.take(spots, (slots + first) % home, axis=0)
    rest = jnp.take(spots, (slots + first + second) % home, axis=0)
    early = subzone_pass(fields, modulus[None], spots, first[None], HALO, extent)
    data = jnp.concatenate([fields, modulus[None]], axis=0)
    extended = with_halo(data, (("vy", 2), ("vx", 1)), HALO)
    total = subzone_pass(extended, extended, middle_spots, second[None], 0, extent)
    late = subzone_pass(extended, extended, rest, (count - first - second)[None], 0, extent)
    from_above = passed_along(total[:HALO], "vx", -1)
    from_below = passed_along(total[TX + HALO :], "vx", 1)
    middle = total[HALO : HALO + TX] + late[HALO : HALO + TX] + early[HALO : HALO + TX]
    middle = middle.at[:HALO].add(from_below).at[TX - HALO :].add(from_above)
    from_right = passed_along(middle[:, :HALO], "vy", -1)
    from_left = passed_along(middle[:, TY + HALO :], "vy", 1)
    owned = middle[:, HALO : HALO + TY]
    owned = owned.at[:, :HALO].add(from_left).at[:, TY - HALO :].add(from_right)
    return owned


def solution(mesh):
    return jax.shard_map(
        shards,
        mesh=mesh,
        in_specs=(
            P(None, "vx", "vy", None),
            P("vx", "vy", None),
            P("vx", "vy", None, None),
            P("vx", "vy"),
        ),
        out_specs=P("vx", "vy", None),
        check_vma=False,
    )
```

```python
import functools

import jax
import jax.numpy as jnp
from jax import lax
from jax.experimental import pallas as pl
from jax.experimental.pallas import tpu as pltpu
from jax.sharding import PartitionSpec as P

NF = 4
SUB = 32
HALO = 16
TX = 64
TY = 160
RFWD = 3


OMEGA = 0.07
PADY = 8
STEP_FLOPS = 30_000_000_000
STEP_BYTES = 2 * (NF + 1) * SUB * SUB * 128 * 2


def with_halo(x, sides, width):
    for axis, dim in sides:
        size, length = (lax.axis_size(axis), x.shape[dim])
        up = [(i, (i + 1) % size) for i in range(size - 1)]
        down = [(j, i) for i, j in up]
        last = lax.slice_in_dim(x, length - width, length, axis=dim)
        first = lax.slice_in_dim(x, 0, width, axis=dim)
        before = lax.ppermute(last, axis, up)
        after = lax.ppermute(first, axis, down)
        x = jnp.concatenate([before, x, after], axis=dim)
    return x


def passed_along(x, axis, by):
    length = lax.axis_size(axis)
    pairs = [(i, i + by) for i in range(length) if 0 <= i + by < length]
    return lax.ppermute(x, axis, pairs)


def subzone_kernel(spots_ref, count_ref, block_a, mod_a, block_b, mod_b, total_ref,
                   um_ref, mur_ref, muis_ref, w1_ref, w2_ref, t_ref,
                   img1_ref, s1_ref, v3_ref, p_ref, q_ref):
    step = pl.program_id(0)
    lanes = block_a.shape[-1]
    half = lanes // 2
    group = half // 2
    first = 2 * step
    second = jnp.minimum(first + 1, count_ref[0] - 1)

    @pl.when(step == 0)
    def _():
        total_ref[...] = jnp.zeros_like(total_ref)
        for ref in (w1_ref, w2_ref, t_ref):
            nf, rows, cols, width = ref.shape
            ref[:, 0] = jnp.zeros((nf, cols, width), jnp.float32)
            ref[:, rows - 1] = jnp.zeros((nf, cols, width), jnp.float32)
            ref[:, :, :PADY] = jnp.zeros((nf, rows, PADY, width), jnp.float32)
            ref[:, :, cols - PADY :] = jnp.zeros((nf, rows, PADY, width), jnp.float32)

    @pl.when(first < count_ref[0])
    def _():
        xa = spots_ref[first, 0]
        ya = pl.multiple_of(spots_ref[first, 1], HALO)
        za = spots_ref[first, 2]
        xb = spots_ref[second, 0]
        yb = pl.multiple_of(spots_ref[second, 1], HALO)
        zb = spots_ref[second, 2]
        lane = lax.broadcasted_iota(jnp.int32, (SUB, lanes), 1)
        depth = lane % half
        in_a = (lane % half) < group
        upper = lane >= half
        not_low = (lane % group) != 0
        not_high = (lane % group) != group - 1
        shift_a = (lanes - za) % lanes
        shift_b = (group - zb + lanes) % lanes

        def swap(v):
            return pltpu.roll(v, half, 1)

        def packed(ref_a, ref_b, k, x):
            a = ref_a[k, x].astype(jnp.float32)
            b = ref_b[k, x].astype(jnp.float32)
            return jnp.where(in_a, pltpu.roll(a, shift_a, 1), pltpu.roll(b, shift_b, 1))

        def laplace(ref, f, x):
            c = ref[f, x + 1, PADY:PADY + SUB, :]
            side = ref[f, x, PADY:PADY + SUB, :] + ref[f, x + 2, PADY:PADY + SUB, :]
            side = side + ref[f, x + 1, PADY - 1:PADY - 1 + SUB, :]
            side = side + ref[f, x + 1, PADY + 1:PADY + 1 + SUB, :]
            side = side + jnp.where(not_low, pltpu.roll(c, 1, 1), 0.0)
            side = side + jnp.where(not_high, pltpu.roll(c, lanes - 1, 1), 0.0)
            return 6.0 * c - side, c

        def stage_a(x, carry):
            mu = packed(mod_a, mod_b, 0, x)
            smu = swap(mu)
            mur_ref[x] = jnp.where(upper, smu, mu)
            muis_ref[x] = jnp.where(upper, mu, -smu)
            for f in range(NF):
                u = packed(block_a, block_b, f, x)
                um_ref[f, x] = u
                w1_ref[f, x + 1, PADY:PADY + SUB, :] = OMEGA * u
            return carry

        lax.fori_loop(0, SUB, stage_a, 0)

        def stage_b(x, carry):
            mur = mur_ref[x]
            muis = muis_ref[x]
            for f in range(NF):
                img, c = laplace(w1_ref, f, x)
                s = swap(img)
                u = um_ref[f, x]
                w2_ref[f, x + 1, PADY:PADY + SUB, :] = c + OMEGA * (u - c - (mur * img + muis * s))
                img1_ref[f, x] = img
                s1_ref[f, x] = s
            return carry

        lax.fori_loop(0, SUB, stage_b, 0)

        def stage_c(x, carry):
            mur = mur_ref[x]
            muis = muis_ref[x]
            pacc = jnp.zeros((SUB, lanes), jnp.float32)
            qacc = jnp.zeros((SUB, lanes), jnp.float32)
            for f in range(NF):
                img, c = laplace(w2_ref, f, x)
                s = swap(img)
                u = um_ref[f, x]
                w3 = c + OMEGA * (u - c - (mur * img + muis * s))
                v3 = w3 - u
                t_ref[f, x + 1, PADY:PADY + SUB, :] = mur * v3 - muis * swap(v3)
                v3_ref[f, x] = v3
                pacc = pacc + v3 * img
                qacc = qacc + v3 * s
            p_ref[x] = pacc
            q_ref[x] = qacc
            return carry

        lax.fori_loop(0, SUB, stage_c, 0)

        window_a = (depth >= za) & (depth < za + SUB)
        window_b = (depth >= zb) & (depth < zb + SUB)
        back_a = za % lanes
        back_b = (zb + lanes - group) % lanes
        live_b = first + 1 < count_ref[0]

        def stage_d(x, carry):
            pacc = p_ref[x]
            qacc = q_ref[x]
            for f in range(NF):
                lt, _ = laplace(t_ref, f, x)
                v3 = v3_ref[f, x]
                v2 = v3 - OMEGA * (v3 + lt)
                pacc = pacc + v2 * img1_ref[f, x]
                qacc = qacc + v2 * s1_ref[f, x]
            res = -OMEGA * jnp.where(upper, qacc - swap(qacc), pacc + swap(pacc))
            total_ref[xa + x, pl.ds(ya, SUB), :] += jnp.where(window_a, pltpu.roll(res, back_a, 1), 0.0)

            @pl.when(live_b)
            def _():
                total_ref[xb + x, pl.ds(yb, SUB), :] += jnp.where(window_b, pltpu.roll(res, back_b, 1), 0.0)

            return carry

        lax.fori_loop(0, SUB, stage_d, 0)


def subzone_pass(fields, modulus, spots, count, shift, extent):
    lanes = fields.shape[-1]
    home = spots.shape[0]
    ex, ey = extent

    def block_map(offset, base):
        def index(s, spots_ref, count_ref):
            live = jnp.minimum(2 * s + offset, jnp.maximum(count_ref[0] - 1, 0))
            row = jnp.clip(spots_ref[live, 0] - shift, 0, fields.shape[1] - SUB)
            col = jnp.clip(spots_ref[live, 1] - shift, 0, fields.shape[2] - SUB)
            col = pl.multiple_of(col, HALO)
            return (base, row, col, 0)
        return index

    f32 = jnp.float32
    padded = (NF, SUB + 2, SUB + 2 * PADY, lanes)
    block = (pl.Element(NF), pl.Element(SUB), pl.Element(SUB), pl.Element(lanes))
    mod_block = (pl.Element(1), pl.Element(SUB), pl.Element(SUB), pl.Element(lanes))
    base = modulus.shape[0] - 1
    grid_spec = pltpu.PrefetchScalarGridSpec(
        num_scalar_prefetch=2,
        grid=((home + 1) // 2,),
        in_specs=[
            pl.BlockSpec(block, block_map(0, 0)),
            pl.BlockSpec(mod_block, block_map(0, base)),
            pl.BlockSpec(block, block_map(1, 0)),
            pl.BlockSpec(mod_block, block_map(1, base)),
        ],
        out_specs=pl.BlockSpec((ex, ey, lanes), lambda s, spots_ref, count_ref: (0, 0, 0)),
        scratch_shapes=[
            pltpu.VMEM((NF, SUB, SUB, lanes), f32),
            pltpu.VMEM((SUB, SUB, lanes), f32),
            pltpu.VMEM((SUB, SUB, lanes), f32),
            pltpu.VMEM(padded, f32),
            pltpu.VMEM(padded, f32),
            pltpu.VMEM(padded, f32),
            pltpu.VMEM((NF, SUB, SUB, lanes), f32),
            pltpu.VMEM((NF, SUB, SUB, lanes), f32),
            pltpu.VMEM((NF, SUB, SUB, lanes), f32),
            pltpu.VMEM((SUB, SUB, lanes), f32),
            pltpu.VMEM((SUB, SUB, lanes), f32),
        ],
    )
    return pl.pallas_call(
        subzone_kernel,
        grid_spec=grid_spec,
        out_shape=jax.ShapeDtypeStruct((ex, ey, lanes), f32),
        cost_estimate=pl.CostEstimate(
            flops=STEP_FLOPS * ((home + 1) // 2), transcendentals=0, bytes_accessed=STEP_BYTES * ((home + 1) // 2)
        ),
        compiler_params=pltpu.CompilerParams(
            dimension_semantics=("arbitrary",), vmem_limit_bytes=100 * 1024 * 1024
        ),
    )(spots, count, fields, modulus, fields, modulus)


def shards(fields, modulus, anchors, home_count):
    home = anchors.shape[2]
    extent = (TX + 2 * HALO, TY + 2 * HALO)
    spots = (anchors[0, 0] * HALO).astype(jnp.int32)
    count = home_count[0, 0].astype(jnp.int32)
    slots = jnp.arange(home, dtype=jnp.int32)
    live = slots < count
    edge = ((spots[:, 0] < HALO) | (spots[:, 0] + SUB > TX + HALO)) & live
    side = (spots[:, 1] < HALO) | (spots[:, 1] + SUB > TY + HALO)
    inner = live & ~edge & ~side
    key = jnp.where(inner, 0, jnp.where(edge, 1, jnp.where(live, 2, 3)))
    order = jnp.argsort(key.astype(jnp.int32), stable=True)
    spots = spots[order]
    n_inner = jnp.sum(inner.astype(jnp.int32))
    n_edge = jnp.sum(edge.astype(jnp.int32))
    first = (n_inner // 2) * 2
    second = n_edge + n_inner % 2
    second = jnp.minimum(second + second % 2, count - first)
    middle_spots = jnp.take(spots, (slots + first) % home, axis=0)
    rest = jnp.take(spots, (slots + first + second) % home, axis=0)
    early = subzone_pass(fields, modulus[None], spots, first[None], HALO, extent)
    data = jnp.concatenate([fields, modulus[None]], axis=0)
    extended = with_halo(data, (("vy", 2), ("vx", 1)), HALO)
    total = subzone_pass(extended, extended, middle_spots, second[None], 0, extent)
    late = subzone_pass(extended, extended, rest, (count - first - second)[None], 0, extent)
    from_above = passed_along(total[:HALO], "vx", -1)
    from_below = passed_along(total[TX + HALO :], "vx", 1)
    middle = total[HALO : HALO + TX] + late[HALO : HALO + TX] + early[HALO : HALO + TX]
    middle = middle.at[:HALO].add(from_below).at[TX - HALO :].add(from_above)
    from_right = passed_along(middle[:, :HALO], "vy", -1)
    from_left = passed_along(middle[:, TY + HALO :], "vy", 1)
    owned = middle[:, HALO : HALO + TY]
    owned = owned.at[:, :HALO].add(from_left).at[:, TY - HALO :].add(from_right)
    return owned


def solution(mesh):
    return jax.shard_map(
        shards,
        mesh=mesh,
        in_specs=(
            P(None, "vx", "vy", None),
            P("vx", "vy", None),
            P("vx", "vy", None, None),
            P("vx", "vy"),
        ),
        out_specs=P("vx", "vy", None),
        check_vma=False,
    )
```

```python
import functools

import jax
import jax.numpy as jnp
from jax import lax
from jax.experimental import pallas as pl
from jax.experimental.pallas import tpu as pltpu
from jax.sharding import PartitionSpec as P

NF = 4
SUB = 32
HALO = 16
TX = 64
TY = 160
RFWD = 3


OMEGA = 0.07
PADY = 8
STEP_FLOPS = 30_000_000_000
STEP_BYTES = 2 * (NF + 1) * SUB * SUB * 128 * 2


def with_halo(x, sides, width):
    for axis, dim in sides:
        size, length = (lax.axis_size(axis), x.shape[dim])
        up = [(i, (i + 1) % size) for i in range(size - 1)]
        down = [(j, i) for i, j in up]
        last = lax.slice_in_dim(x, length - width, length, axis=dim)
        first = lax.slice_in_dim(x, 0, width, axis=dim)
        before = lax.ppermute(last, axis, up)
        after = lax.ppermute(first, axis, down)
        x = jnp.concatenate([before, x, after], axis=dim)
    return x


def passed_along(x, axis, by):
    length = lax.axis_size(axis)
    pairs = [(i, i + by) for i in range(length) if 0 <= i + by < length]
    return lax.ppermute(x, axis, pairs)


def subzone_kernel(spots_ref, count_ref, block_a, mod_a, block_b, mod_b, total_ref,
                   um_ref, mur_ref, muis_ref, w1_ref, w2_ref, t_ref,
                   img1_ref, s1_ref, v3_ref, p_ref, q_ref):
    step = pl.program_id(0)
    lanes = block_a.shape[-1]
    half = lanes // 2
    group = half // 2
    first = 2 * step
    second = jnp.minimum(first + 1, count_ref[0] - 1)

    @pl.when(step == 0)
    def _():
        total_ref[...] = jnp.zeros_like(total_ref)
        w1_ref[...] = jnp.zeros_like(w1_ref)
        w2_ref[...] = jnp.zeros_like(w2_ref)
        t_ref[...] = jnp.zeros_like(t_ref)

    @pl.when(first < count_ref[0])
    def _():
        xa = spots_ref[first, 0]
        ya = pl.multiple_of(spots_ref[first, 1], HALO)
        za = spots_ref[first, 2]
        xb = spots_ref[second, 0]
        yb = pl.multiple_of(spots_ref[second, 1], HALO)
        zb = spots_ref[second, 2]
        lane = lax.broadcasted_iota(jnp.int32, (SUB, lanes), 1)
        depth = lane % half
        in_a = (lane % half) < group
        upper = lane >= half
        not_low = (lane % group) != 0
        not_high = (lane % group) != group - 1
        shift_a = (lanes - za) % lanes
        shift_b = (group - zb + lanes) % lanes

        def swap(v):
            return pltpu.roll(v, half, 1)

        def packed(ref_a, ref_b, k, x):
            a = ref_a[k, x].astype(jnp.float32)
            b = ref_b[k, x].astype(jnp.float32)
            return jnp.where(in_a, pltpu.roll(a, shift_a, 1), pltpu.roll(b, shift_b, 1))

        def laplace(ref, f, x):
            c = ref[f, x + 1, PADY:PADY + SUB, :]
            side = ref[f, x, PADY:PADY + SUB, :] + ref[f, x + 2, PADY:PADY + SUB, :]
            side = side + ref[f, x + 1, PADY - 1:PADY - 1 + SUB, :]
            side = side + ref[f, x + 1, PADY + 1:PADY + 1 + SUB, :]
            side = side + jnp.where(not_low, pltpu.roll(c, 1, 1), 0.0)
            side = side + jnp.where(not_high, pltpu.roll(c, lanes - 1, 1), 0.0)
            return 6.0 * c - side, c

        def stage_a(x, carry):
            mu = packed(mod_a, mod_b, 0, x)
            smu = swap(mu)
            mur_ref[x] = jnp.where(upper, smu, mu)
            muis_ref[x] = jnp.where(upper, mu, -smu)
            for f in range(NF):
                u = packed(block_a, block_b, f, x)
                um_ref[f, x] = u
                w1_ref[f, x + 1, PADY:PADY + SUB, :] = OMEGA * u
            return carry

        lax.fori_loop(0, SUB, stage_a, 0)

        def stage_b(x, carry):
            mur = mur_ref[x]
            muis = muis_ref[x]
            for f in range(NF):
                img, c = laplace(w1_ref, f, x)
                s = swap(img)
                u = um_ref[f, x]
                w2_ref[f, x + 1, PADY:PADY + SUB, :] = c + OMEGA * (u - c - (mur * img + muis * s))
                img1_ref[f, x] = img
                s1_ref[f, x] = s
            return carry

        lax.fori_loop(0, SUB, stage_b, 0)

        def stage_c(x, carry):
            mur = mur_ref[x]
            muis = muis_ref[x]
            pacc = jnp.zeros((SUB, lanes), jnp.float32)
            qacc = jnp.zeros((SUB, lanes), jnp.float32)
            for f in range(NF):
                img, c = laplace(w2_ref, f, x)
                s = swap(img)
                u = um_ref[f, x]
                w3 = c + OMEGA * (u - c - (mur * img + muis * s))
                v3 = w3 - u
                t_ref[f, x + 1, PADY:PADY + SUB, :] = mur * v3 - muis * swap(v3)
                v3_ref[f, x] = v3
                pacc = pacc + v3 * img
                qacc = qacc + v3 * s
            p_ref[x] = pacc
            q_ref[x] = qacc
            return carry

        lax.fori_loop(0, SUB, stage_c, 0)

        window_a = (depth >= za) & (depth < za + SUB)
        window_b = (depth >= zb) & (depth < zb + SUB)
        back_a = za % lanes
        back_b = (zb + lanes - group) % lanes
        live_b = first + 1 < count_ref[0]

        def stage_d(x, carry):
            pacc = p_ref[x]
            qacc = q_ref[x]
            for f in range(NF):
                lt, _ = laplace(t_ref, f, x)
                v3 = v3_ref[f, x]
                v2 = v3 - OMEGA * (v3 + lt)
                pacc = pacc + v2 * img1_ref[f, x]
                qacc = qacc + v2 * s1_ref[f, x]
            res = -OMEGA * jnp.where(upper, qacc - swap(qacc), pacc + swap(pacc))
            total_ref[xa + x, pl.ds(ya, SUB), :] += jnp.where(window_a, pltpu.roll(res, back_a, 1), 0.0)

            @pl.when(live_b)
            def _():
                total_ref[xb + x, pl.ds(yb, SUB), :] += jnp.where(window_b, pltpu.roll(res, back_b, 1), 0.0)

            return carry

        lax.fori_loop(0, SUB, stage_d, 0)


def subzone_pass(fields, modulus, spots, count, shift, extent):
    lanes = fields.shape[-1]
    home = spots.shape[0]
    ex, ey = extent

    def block_map(offset, base):
        def index(s, spots_ref, count_ref):
            live = jnp.minimum(2 * s + offset, jnp.maximum(count_ref[0] - 1, 0))
            row = jnp.clip(spots_ref[live, 0] - shift, 0, fields.shape[1] - SUB)
            col = jnp.clip(spots_ref[live, 1] - shift, 0, fields.shape[2] - SUB)
            col = pl.multiple_of(col, HALO)
            return (base, row, col, 0)
        return index

    f32 = jnp.float32
    padded = (NF, SUB + 2, SUB + 2 * PADY, lanes)
    block = (pl.Element(NF), pl.Element(SUB), pl.Element(SUB), pl.Element(lanes))
    mod_block = (pl.Element(1), pl.Element(SUB), pl.Element(SUB), pl.Element(lanes))
    base = modulus.shape[0] - 1
    grid_spec = pltpu.PrefetchScalarGridSpec(
        num_scalar_prefetch=2,
        grid=((home + 1) // 2,),
        in_specs=[
            pl.BlockSpec(block, block_map(0, 0)),
            pl.BlockSpec(mod_block, block_map(0, base)),
            pl.BlockSpec(block, block_map(1, 0)),
            pl.BlockSpec(mod_block, block_map(1, base)),
        ],
        out_specs=pl.BlockSpec((ex, ey, lanes), lambda s, spots_ref, count_ref: (0, 0, 0)),
        scratch_shapes=[
            pltpu.VMEM((NF, SUB, SUB, lanes), f32),
            pltpu.VMEM((SUB, SUB, lanes), f32),
            pltpu.VMEM((SUB, SUB, lanes), f32),
            pltpu.VMEM(padded, f32),
            pltpu.VMEM(padded, f32),
            pltpu.VMEM(padded, f32),
            pltpu.VMEM((NF, SUB, SUB, lanes), f32),
            pltpu.VMEM((NF, SUB, SUB, lanes), f32),
            pltpu.VMEM((NF, SUB, SUB, lanes), f32),
            pltpu.VMEM((SUB, SUB, lanes), f32),
            pltpu.VMEM((SUB, SUB, lanes), f32),
        ],
    )
    return pl.pallas_call(
        subzone_kernel,
        grid_spec=grid_spec,
        out_shape=jax.ShapeDtypeStruct((ex, ey, lanes), f32),
        cost_estimate=pl.CostEstimate(
            flops=STEP_FLOPS * ((home + 1) // 2), transcendentals=0, bytes_accessed=STEP_BYTES * ((home + 1) // 2)
        ),
        compiler_params=pltpu.CompilerParams(
            dimension_semantics=("arbitrary",), vmem_limit_bytes=100 * 1024 * 1024
        ),
    )(spots, count, fields, modulus, fields, modulus)


def shards(fields, modulus, anchors, home_count):
    home = anchors.shape[2]
    extent = (TX + 2 * HALO, TY + 2 * HALO)
    spots = (anchors[0, 0] * HALO).astype(jnp.int32)
    count = home_count[0, 0].astype(jnp.int32)
    slots = jnp.arange(home, dtype=jnp.int32)
    live = slots < count
    edge = ((spots[:, 0] < HALO) | (spots[:, 0] + SUB > TX + HALO)) & live
    side = (spots[:, 1] < HALO) | (spots[:, 1] + SUB > TY + HALO)
    inner = live & ~edge & ~side
    key = jnp.where(inner, 0, jnp.where(edge, 1, jnp.where(live, 2, 3)))
    order = jnp.argsort(key.astype(jnp.int32), stable=True)
    spots = spots[order]
    n_inner = jnp.sum(inner.astype(jnp.int32))
    n_edge = jnp.sum(edge.astype(jnp.int32))
    first = (n_inner // 2) * 2
    second = n_edge + n_inner % 2
    second = jnp.minimum(second + second % 2, count - first)
    middle_spots = jnp.take(spots, (slots + first) % home, axis=0)
    rest = jnp.take(spots, (slots + first + second) % home, axis=0)
    early = subzone_pass(fields, modulus[None], spots, first[None], HALO, extent)
    data = jnp.concatenate([fields, modulus[None]], axis=0)
    ylo = passed_along(data[:, :, TY - HALO :], "vy", 1)
    yhi = passed_along(data[:, :, :HALO], "vy", -1)

    def band(rows):
        return jnp.concatenate([ylo[:, rows], data[:, rows], yhi[:, rows]], axis=2)

    xlo = passed_along(band(slice(TX - HALO, TX)), "vx", 1)
    xhi = passed_along(band(slice(0, HALO)), "vx", -1)
    wide = jnp.concatenate([ylo, data, yhi], axis=2)
    extended = jnp.concatenate([xlo, wide, xhi], axis=1)
    total = subzone_pass(extended, extended, middle_spots, second[None], 0, extent)
    late = subzone_pass(extended, extended, rest, (count - first - second)[None], 0, extent)
    from_above = passed_along(total[:HALO], "vx", -1)
    from_below = passed_along(total[TX + HALO :], "vx", 1)
    middle = total[HALO : HALO + TX] + late[HALO : HALO + TX] + early[HALO : HALO + TX]
    middle = middle.at[:HALO].add(from_below).at[TX - HALO :].add(from_above)
    from_right = passed_along(middle[:, :HALO], "vy", -1)
    from_left = passed_along(middle[:, TY + HALO :], "vy", 1)
    owned = middle[:, HALO : HALO + TY]
    owned = owned.at[:, :HALO].add(from_left).at[:, TY - HALO :].add(from_right)
    return owned


def solution(mesh):
    return jax.shard_map(
        shards,
        mesh=mesh,
        in_specs=(
            P(None, "vx", "vy", None),
            P("vx", "vy", None),
            P("vx", "vy", None, None),
            P("vx", "vy"),
        ),
        out_specs=P("vx", "vy", None),
        check_vma=False,
    )
```

```python
import functools

import jax
import jax.numpy as jnp
from jax import lax
from jax.experimental import pallas as pl
from jax.experimental.pallas import tpu as pltpu
from jax.sharding import PartitionSpec as P

NF = 4
SUB = 32
HALO = 16
TX = 64
TY = 160
RFWD = 3


OMEGA = 0.07
PADY = 8
STEP_FLOPS = 30_000_000_000
STEP_BYTES = 2 * (NF + 1) * SUB * SUB * 128 * 2


def with_halo(x, sides, width):
    for axis, dim in sides:
        size, length = (lax.axis_size(axis), x.shape[dim])
        up = [(i, (i + 1) % size) for i in range(size - 1)]
        down = [(j, i) for i, j in up]
        last = lax.slice_in_dim(x, length - width, length, axis=dim)
        first = lax.slice_in_dim(x, 0, width, axis=dim)
        before = lax.ppermute(last, axis, up)
        after = lax.ppermute(first, axis, down)
        x = jnp.concatenate([before, x, after], axis=dim)
    return x


def passed_along(x, axis, by):
    length = lax.axis_size(axis)
    pairs = [(i, i + by) for i in range(length) if 0 <= i + by < length]
    return lax.ppermute(x, axis, pairs)


def subzone_kernel(spots_ref, count_ref, block_a, mod_a, block_b, mod_b, total_ref,
                   um_ref, mur_ref, muis_ref, w1_ref, w2_ref, t_ref,
                   img1_ref, s1_ref, v3_ref, p_ref, q_ref):
    step = pl.program_id(0)
    lanes = block_a.shape[-1]
    half = lanes // 2
    group = half // 2
    first = 2 * step
    second = jnp.minimum(first + 1, count_ref[0] - 1)

    @pl.when(step == 0)
    def _():
        total_ref[...] = jnp.zeros_like(total_ref)
        for ref in (w1_ref, w2_ref, t_ref):
            nf, rows, cols, width = ref.shape
            ref[:, 0] = jnp.zeros((nf, cols, width), jnp.float32)
            ref[:, rows - 1] = jnp.zeros((nf, cols, width), jnp.float32)
            ref[:, :, :PADY] = jnp.zeros((nf, rows, PADY, width), jnp.float32)
            ref[:, :, cols - PADY :] = jnp.zeros((nf, rows, PADY, width), jnp.float32)

    @pl.when(first < count_ref[0])
    def _():
        xa = spots_ref[first, 0]
        ya = pl.multiple_of(spots_ref[first, 1], HALO)
        za = spots_ref[first, 2]
        xb = spots_ref[second, 0]
        yb = pl.multiple_of(spots_ref[second, 1], HALO)
        zb = spots_ref[second, 2]
        lane = lax.broadcasted_iota(jnp.int32, (SUB, lanes), 1)
        depth = lane % half
        in_a = (lane % half) < group
        upper = lane >= half
        not_low = (lane % group) != 0
        not_high = (lane % group) != group - 1
        shift_a = (lanes - za) % lanes
        shift_b = (group - zb + lanes) % lanes

        def swap(v):
            return pltpu.roll(v, half, 1)

        def packed(ref_a, ref_b, k, x):
            a = ref_a[k, x].astype(jnp.float32)
            b = ref_b[k, x].astype(jnp.float32)
            return jnp.where(in_a, pltpu.roll(a, shift_a, 1), pltpu.roll(b, shift_b, 1))

        def laplace(ref, f, x):
            c = ref[f, x + 1, PADY:PADY + SUB, :]
            side = ref[f, x, PADY:PADY + SUB, :] + ref[f, x + 2, PADY:PADY + SUB, :]
            side = side + ref[f, x + 1, PADY - 1:PADY - 1 + SUB, :]
            side = side + ref[f, x + 1, PADY + 1:PADY + 1 + SUB, :]
            side = side + jnp.where(not_low, pltpu.roll(c, 1, 1), 0.0)
            side = side + jnp.where(not_high, pltpu.roll(c, lanes - 1, 1), 0.0)
            return 6.0 * c - side, c

        def stage_a(x, carry):
            mu = packed(mod_a, mod_b, 0, x)
            smu = swap(mu)
            mur_ref[x] = jnp.where(upper, smu, mu)
            muis_ref[x] = jnp.where(upper, mu, -smu)
            for f in range(NF):
                u = packed(block_a, block_b, f, x)
                um_ref[f, x] = u
                w1_ref[f, x + 1, PADY:PADY + SUB, :] = OMEGA * u
            return carry

        lax.fori_loop(0, SUB, stage_a, 0)

        def stage_b(x, carry):
            mur = mur_ref[x]
            muis = muis_ref[x]
            for f in range(NF):
                img, c = laplace(w1_ref, f, x)
                s = swap(img)
                u = um_ref[f, x]
                w2_ref[f, x + 1, PADY:PADY + SUB, :] = c + OMEGA * (u - c - (mur * img + muis * s))
                img1_ref[f, x] = img
                s1_ref[f, x] = s
            return carry

        lax.fori_loop(0, SUB, stage_b, 0)

        def stage_c(x, carry):
            mur = mur_ref[x]
            muis = muis_ref[x]
            pacc = jnp.zeros((SUB, lanes), jnp.float32)
            qacc = jnp.zeros((SUB, lanes), jnp.float32)
            for f in range(NF):
                img, c = laplace(w2_ref, f, x)
                s = swap(img)
                u = um_ref[f, x]
                w3 = c + OMEGA * (u - c - (mur * img + muis * s))
                v3 = w3 - u
                t_ref[f, x + 1, PADY:PADY + SUB, :] = mur * v3 - muis * swap(v3)
                v3_ref[f, x] = v3
                pacc = pacc + v3 * img
                qacc = qacc + v3 * s
            p_ref[x] = pacc
            q_ref[x] = qacc
            return carry

        lax.fori_loop(0, SUB, stage_c, 0)

        window_a = (depth >= za) & (depth < za + SUB)
        window_b = (depth >= zb) & (depth < zb + SUB)
        back_a = za % lanes
        back_b = (zb + lanes - group) % lanes
        live_b = first + 1 < count_ref[0]

        def stage_d(x, carry):
            pacc = p_ref[x]
            qacc = q_ref[x]
            for f in range(NF):
                lt, _ = laplace(t_ref, f, x)
                v3 = v3_ref[f, x]
                v2 = v3 - OMEGA * (v3 + lt)
                pacc = pacc + v2 * img1_ref[f, x]
                qacc = qacc + v2 * s1_ref[f, x]
            res = -OMEGA * jnp.where(upper, qacc - swap(qacc), pacc + swap(pacc))
            total_ref[xa + x, pl.ds(ya, SUB), :] += jnp.where(window_a, pltpu.roll(res, back_a, 1), 0.0)

            @pl.when(live_b)
            def _():
                total_ref[xb + x, pl.ds(yb, SUB), :] += jnp.where(window_b, pltpu.roll(res, back_b, 1), 0.0)

            return carry

        lax.fori_loop(0, SUB, stage_d, 0)


def subzone_pass(fields, modulus, spots, count, shift, extent):
    lanes = fields.shape[-1]
    home = spots.shape[0]
    ex, ey = extent

    def block_map(offset, base):
        def index(s, spots_ref, count_ref):
            live = jnp.minimum(2 * s + offset, jnp.maximum(count_ref[0] - 1, 0))
            row = jnp.clip(spots_ref[live, 0] - shift, 0, fields.shape[1] - SUB)
            col = jnp.clip(spots_ref[live, 1] - shift, 0, fields.shape[2] - SUB)
            col = pl.multiple_of(col, HALO)
            return (base, row, col, 0)
        return index

    f32 = jnp.float32
    padded = (NF, SUB + 2, SUB + 2 * PADY, lanes)
    block = (pl.Element(NF), pl.Element(SUB), pl.Element(SUB), pl.Element(lanes))
    mod_block = (pl.Element(1), pl.Element(SUB), pl.Element(SUB), pl.Element(lanes))
    base = modulus.shape[0] - 1
    grid_spec = pltpu.PrefetchScalarGridSpec(
        num_scalar_prefetch=2,
        grid=((home + 1) // 2,),
        in_specs=[
            pl.BlockSpec(block, block_map(0, 0)),
            pl.BlockSpec(mod_block, block_map(0, base)),
            pl.BlockSpec(block, block_map(1, 0)),
            pl.BlockSpec(mod_block, block_map(1, base)),
        ],
        out_specs=pl.BlockSpec((ex, ey, lanes), lambda s, spots_ref, count_ref: (0, 0, 0)),
        scratch_shapes=[
            pltpu.VMEM((NF, SUB, SUB, lanes), f32),
            pltpu.VMEM((SUB, SUB, lanes), f32),
            pltpu.VMEM((SUB, SUB, lanes), f32),
            pltpu.VMEM(padded, f32),
            pltpu.VMEM(padded, f32),
            pltpu.VMEM(padded, f32),
            pltpu.VMEM((NF, SUB, SUB, lanes), f32),
            pltpu.VMEM((NF, SUB, SUB, lanes), f32),
            pltpu.VMEM((NF, SUB, SUB, lanes), f32),
            pltpu.VMEM((SUB, SUB, lanes), f32),
            pltpu.VMEM((SUB, SUB, lanes), f32),
        ],
    )
    return pl.pallas_call(
        subzone_kernel,
        grid_spec=grid_spec,
        out_shape=jax.ShapeDtypeStruct((ex, ey, lanes), f32),
        cost_estimate=pl.CostEstimate(
            flops=STEP_FLOPS * ((home + 1) // 2), transcendentals=0, bytes_accessed=STEP_BYTES * ((home + 1) // 2)
        ),
        compiler_params=pltpu.CompilerParams(
            dimension_semantics=("arbitrary",), vmem_limit_bytes=100 * 1024 * 1024
        ),
    )(spots, count, fields, modulus, fields, modulus)


def shards(fields, modulus, anchors, home_count):
    home = anchors.shape[2]
    extent = (TX + 2 * HALO, TY + 2 * HALO)
    spots = (anchors[0, 0] * HALO).astype(jnp.int32)
    count = home_count[0, 0].astype(jnp.int32)
    slots = jnp.arange(home, dtype=jnp.int32)
    live = slots < count
    edge = ((spots[:, 0] < HALO) | (spots[:, 0] + SUB > TX + HALO)) & live
    side = (spots[:, 1] < HALO) | (spots[:, 1] + SUB > TY + HALO)
    inner = live & ~edge & ~side
    key = jnp.where(inner, 0, jnp.where(edge, 1, jnp.where(live, 2, 3)))
    order = jnp.argsort(key.astype(jnp.int32), stable=True)
    spots = spots[order]
    n_inner = jnp.sum(inner.astype(jnp.int32))
    n_edge = jnp.sum(edge.astype(jnp.int32))
    first = (n_inner // 2) * 2
    second = n_edge + n_inner % 2
    second = jnp.minimum(second + second % 2, count - first)
    middle_spots = jnp.take(spots, (slots + first) % home, axis=0)
    rest = jnp.take(spots, (slots + first + second) % home, axis=0)
    early = subzone_pass(fields, modulus[None], spots, first[None], HALO, extent)
    data = jnp.concatenate([fields, modulus[None]], axis=0)
    ylo = passed_along(data[:, :, TY - HALO :], "vy", 1)
    yhi = passed_along(data[:, :, :HALO], "vy", -1)

    def band(rows):
        return jnp.concatenate([ylo[:, rows], data[:, rows], yhi[:, rows]], axis=2)

    xlo = passed_along(band(slice(TX - HALO, TX)), "vx", 1)
    xhi = passed_along(band(slice(0, HALO)), "vx", -1)
    wide = jnp.concatenate([ylo, data, yhi], axis=2)
    extended = jnp.concatenate([xlo, wide, xhi], axis=1)
    total = subzone_pass(extended, extended, middle_spots, second[None], 0, extent)
    late = subzone_pass(extended, extended, rest, (count - first - second)[None], 0, extent)
    from_above = passed_along(total[:HALO], "vx", -1)
    from_below = passed_along(total[TX + HALO :], "vx", 1)
    middle = total[HALO : HALO + TX] + late[HALO : HALO + TX] + early[HALO : HALO + TX]
    middle = middle.at[:HALO].add(from_below).at[TX - HALO :].add(from_above)
    from_right = passed_along(middle[:, :HALO], "vy", -1)
    from_left = passed_along(middle[:, TY + HALO :], "vy", 1)
    owned = middle[:, HALO : HALO + TY]
    owned = owned.at[:, :HALO].add(from_left).at[:, TY - HALO :].add(from_right)
    return owned


def solution(mesh):
    return jax.shard_map(
        shards,
        mesh=mesh,
        in_specs=(
            P(None, "vx", "vy", None),
            P("vx", "vy", None),
            P("vx", "vy", None, None),
            P("vx", "vy"),
        ),
        out_specs=P("vx", "vy", None),
        check_vma=False,
    )
```
